32 devices in a mesh: groups: 2 (over y), seq: 4 (over z), chan: 4 (over x, core).
Axes of the slice: x: 2, y: 2, z: 4, core: 2. Of those that a mesh axis runs over, the one named last changes fastest.
Arguments:
- value: bfloat16 [1024, 4096], P(('groups', 'seq'), 'chan'), parts along dimension 0, may hold values from -6 to 6
- first_gate: bfloat16 [1024, 4096], P(('groups', 'seq'), 'chan'), parts along dimension 0, may hold values from -6 to 6
- second_gate: bfloat16 [1024, 4096], P(('groups', 'seq'), 'chan'), parts along dimension 0, may hold values from -6 to 6
- first_filter: bfloat16 [256, 512], P('chan'), may hold values from -0.25 to 0.25
- second_filter: bfloat16 [256, 512], P('chan'), may hold values from -0.25 to 0.25
- out_weight: bfloat16 [4096, 4096], P('chan'), may hold values from -0.09375 to 0.09375
- segment_ids: int32 [1024], P(('groups', 'seq')), parts along dimension 0, may hold values from 0 to 1, never falling along the last dimension, each value on 1 to 384 neighbouring positions
Outputs:
- mixed: bfloat16 [1024, 4096], P(('groups', 'seq')), parts along dimension 0
The draws below stay inside these ranges and needn't reach their ends.
There are 2 independent parts, one for each index of `groups`. The reference program is written for one: setup_inputs(seed, part) draws one part's arguments, and reference() takes and returns one part's arrays. A program takes and returns all parts, laid end to end along the dimension named above; an argument that names none is the same for every part. Nothing has to cross between parts.
Inputs may be any that keep to these rules, and one draw needn't show every extreme that they name: `segment_ids`: ids never fall along the window; the 2 contexts each hold 128 to 384 neighbouring positions and together fill the window.
All inputs are finite; a program needn't handle non-finite values.
Results may differ from the reference program's by a relative error of at most 0.0065.
Values may be sent and summed in bfloat16 or wider, within the bound.
No kernel may reach another device: no remote copies, remote signals or barrier semaphores. Data moves between devices by JAX's collectives and lax.ppermute only.
A program may use at most 192 MiB of HBM per device.

```python
import math
import jax
import jax.numpy as jnp
import numpy as np

D = 4096
FILT_GROUP = 16
FILTERS = 256
SEQ_LEN = 512
SEGMENTS = 2
MOST = 384


def steps_of(key, dims, shards, least, largest):
    loudness = 1.0
    for position, blocks in shards:
        draws = jax.random.uniform(jax.random.fold_in(jax.random.fold_in(key, 6), position), (blocks,), jnp.float32, least / len(shards), largest / len(shards))
        loudness = loudness * jnp.repeat(jnp.exp(draws), dims[position] // blocks).reshape((-1,) + (1,) * (len(dims) - 1 - position))
    return loudness


def profile(amount, total, most, skew):
    weights = [(1 << 20) // math.isqrt(standing ** skew) + 1 for standing in range(2, amount + 1)]
    surplus, holding = total - most - (amount - 1), [1] * (amount - 1)
    while surplus > 0:
        free = [i for i in range(amount - 1) if holding[i] < most]
        pool, budget = sum([weights[i] for i in free]), surplus
        for i in free:
            more = min(most - holding[i], max(1, budget * weights[i] // pool), surplus)
            holding[i] = holding[i] + more
            surplus = surplus - more
    return np.array([most] + holding)


def uneven(key, count, total, most, lean):
    if count == 2:
        one = jax.random.randint(key, (), max(1, total - most), min(most, total - 1) + 1)
        return jnp.stack([one, total - one])
    lengths = jnp.asarray(profile(count, total, most, lean), jnp.int32)
    twos = (count - 1) // 2
    source_of, taker = lengths[1:1 + 2 * twos:2], lengths[2:2 + 2 * twos:2]
    slack = jnp.minimum(source_of - 1, most - taker)
    shifted = jax.random.randint(jax.random.fold_in(key, 1), (twos,), 0, 1 << 20) % (slack + 1)
    lengths = lengths.at[1:1 + 2 * twos:2].set(source_of - shifted).at[2:2 + 2 * twos:2].set(taker + shifted)
    return lengths[jax.random.permutation(jax.random.fold_in(key, 2), count)]


def gaussian(own_key, shape, scale, bound, split=(), dtype=jnp.bfloat16):
    result = scale * jax.random.normal(own_key, shape, jnp.float32)
    if split:
        result = result * steps_of(own_key, shape, split, -0.22, 0.18)
    return jnp.clip(result, -bound, bound).astype(dtype)


def setup_inputs(seed: int = 0, part: int = 0) -> dict:
    seeds = jax.random.split(jax.random.key(seed), 8)
    own_keys = jax.random.split(jax.random.fold_in(seeds[7], part), 8)
    value = gaussian(own_keys[0], (SEQ_LEN, D), 1.0, 6.0, ((0, 4), (1, 4)))
    first_gate = gaussian(own_keys[1], (SEQ_LEN, D), 1.0, 6.0, ((0, 4), (1, 4)))
    second_gate = gaussian(own_keys[2], (SEQ_LEN, D), 1.0, 6.0, ((0, 4), (1, 4)))
    first_filter = gaussian(seeds[3], (FILTERS, SEQ_LEN), SEQ_LEN ** -0.5, 0.25, ((0, 4),))
    second_filter = gaussian(seeds[4], (FILTERS, SEQ_LEN), SEQ_LEN ** -0.5, 0.25, ((0, 4),))
    out_weight = gaussian(seeds[5], (D, D), D ** -0.5, 0.09375, ((0, 4),))
    segment_ids = jnp.searchsorted(jnp.cumsum(uneven(own_keys[6], SEGMENTS, SEQ_LEN, MOST, 0)), jnp.arange(SEQ_LEN), side="right").astype(jnp.int32)
    return dict(value=value, first_gate=first_gate, second_gate=second_gate, first_filter=first_filter, second_filter=second_filter, out_weight=out_weight, segment_ids=segment_ids)


def long_conv(filters, field, segment_ids):
    length, width = field.shape
    spectrum = jnp.fft.rfft(filters.astype(jnp.float32), axis=1)
    spectrum = jnp.repeat(spectrum, FILT_GROUP, axis=0).T
    total = jnp.zeros((length, width), jnp.float32)
    for which in range(SEGMENTS):
        inside = (segment_ids == which).astype(jnp.float32)[:, None]
        masked = field.astype(jnp.float32) * inside
        mixed_part = jnp.fft.irfft(jnp.fft.rfft(masked, axis=0) * spectrum, n=length, axis=0)
        total = total + mixed_part.astype(jnp.float32) * inside
    return total


def reference(value, first_gate, second_gate, first_filter, second_filter, out_weight, segment_ids):
    first_input = (first_gate.astype(jnp.float32) * value.astype(jnp.float32)).astype(jnp.bfloat16)
    first_mix = long_conv(first_filter, first_input, segment_ids)
    second_input = (second_gate.astype(jnp.float32) * first_mix).astype(jnp.bfloat16)
    second_mix = long_conv(second_filter, second_input, segment_ids).astype(jnp.bfloat16)
    return jnp.dot(second_mix, out_weight, preferred_element_type=jnp.float32).astype(jnp.bfloat16)
```

```python
import numpy as np
import jax
import jax.numpy as jnp
from jax import lax
from jax.sharding import PartitionSpec as P

F32 = jnp.float32
BF16 = jnp.bfloat16


def split_bf16(mat):
    hi = mat.astype(jnp.bfloat16)
    lo = (mat - hi.astype(np.float64)).astype(jnp.bfloat16)
    return hi, lo


def dft_mats(length):
    half = length // 2
    n = np.arange(length)
    f = np.arange(half)
    ang = 2.0 * np.pi * ((f[:, None] * n[None, :]) % length) / length
    fwd = np.zeros((length, length))
    fwd[:half] = np.cos(ang)
    fwd[half] = np.where(n % 2 == 0, 1.0, -1.0)
    fwd[half + 1:] = -np.sin(ang[1:])
    inv = np.zeros((length, length))
    scale = np.full(half, 2.0)
    scale[0] = 1.0
    inv[:, :half] = (np.cos(ang) * scale[:, None]).T / length
    inv[:, half] = np.where(n % 2 == 0, 1.0, -1.0) / length
    inv[:, half + 1:] = (-2.0 * np.sin(ang[1:])).T / length
    return split_bf16(fwd), split_bf16(inv)


def mm(a, b):
    return jnp.dot(a, b, preferred_element_type=F32)


def make_local(nseq):
    def local(value, first_gate, second_gate, first_filter, second_filter, out_weight, segment_ids):
        chans = value.shape[1]
        filt_local, length = first_filter.shape
        group = chans // filt_local
        per = chans // nseq
        fpd = per // group
        half = length // 2
        (f_hi, f_lo), (i_hi, i_lo) = dft_mats(length)
        f_hi, f_lo, i_hi, i_lo = (jnp.asarray(m) for m in (f_hi, f_lo, i_hi, i_lo))
        me = lax.axis_index("seq")

        segs = lax.all_gather(segment_ids, "seq", tiled=True)
        in0 = (segs == 0)[:, None]
        in1 = (segs == 1)[:, None]

        def spectrum(filt):
            mine = lax.dynamic_slice_in_dim(filt, me * fpd, fpd, 0)
            taps = jnp.repeat(mine.T, group, axis=1)
            spec = mm(f_hi, taps) + mm(f_lo, taps)
            re, im = spec[:half], spec[half:]
            row0 = lax.broadcasted_iota(jnp.int32, re.shape, 0) == 0
            a = re
            b = jnp.where(row0, 0.0, im)
            d = jnp.where(row0, im, re)
            two = lambda x: jnp.concatenate([x, x], axis=1)
            return two(a), two(b), two(d)

        def long_conv(spec, field):
            a, b, d = spec
            zero = jnp.zeros_like(field)
            masked = jnp.concatenate(
                [jnp.where(in0, field, zero), jnp.where(in1, field, zero)], axis=1
            )
            x = mm(f_hi, masked) + mm(f_lo, masked)
            xr, xi = x[:half], x[half:]
            y = jnp.concatenate([xr * a - xi * b, xr * b + xi * d], axis=0)
            y_hi32 = lax.reduce_precision(y, exponent_bits=8, mantissa_bits=7)
            y_hi = y_hi32.astype(BF16)
            y_lo = (y - y_hi32).astype(BF16)
            both = mm(i_hi, y_hi) + mm(i_hi, y_lo) + mm(i_lo, y_hi)
            return jnp.where(in0, both[:, :per], 0.0) + jnp.where(in1, both[:, per:], 0.0)

        first_input = (first_gate.astype(F32) * value.astype(F32)).astype(BF16)
        first_cols = lax.all_to_all(first_input, "seq", 1, 0, tiled=True)
        gate_cols = lax.all_to_all(second_gate, "seq", 1, 0, tiled=True)
        first_mix = long_conv(spectrum(first_filter), first_cols)
        second_input = (gate_cols.astype(F32) * first_mix).astype(BF16)
        second_mix = long_conv(spectrum(second_filter), second_input).astype(BF16)
        mix_rows = lax.all_to_all(second_mix, "seq", 0, 1, tiled=True)
        partial_out = mm(mix_rows, out_weight)
        return lax.psum(partial_out, "chan").astype(BF16)

    return local


def solution(mesh):
    in_specs = (
        P(("groups", "seq"), "chan"),
        P(("groups", "seq"), "chan"),
        P(("groups", "seq"), "chan"),
        P("chan", None),
        P("chan", None),
        P("chan", None),
        P(("groups", "seq")),
    )
    out_specs = P(("groups", "seq"), None)
    local = make_local(mesh.shape["seq"])
    return jax.shard_map(local, mesh=mesh, in_specs=in_specs, out_specs=out_specs, check_vma=False)
```

```python
import numpy as np
import jax
import jax.numpy as jnp
from jax import lax
from jax.sharding import PartitionSpec as P

F32 = jnp.float32
BF16 = jnp.bfloat16


def split_bf16(mat):
    hi = mat.astype(jnp.bfloat16)
    lo = (mat - hi.astype(np.float64)).astype(jnp.bfloat16)
    return hi, lo


def dft_mats(length):
    half = length // 2
    n = np.arange(length)
    f = np.arange(half)
    ang = 2.0 * np.pi * ((f[:, None] * n[None, :]) % length) / length
    fwd = np.zeros((length, length))
    fwd[:half] = np.cos(ang)
    fwd[half] = np.where(n % 2 == 0, 1.0, -1.0)
    fwd[half + 1:] = -np.sin(ang[1:])
    inv = np.zeros((length, length))
    scale = np.full(half, 2.0)
    scale[0] = 1.0
    inv[:, :half] = (np.cos(ang) * scale[:, None]).T / length
    inv[:, half] = np.where(n % 2 == 0, 1.0, -1.0) / length
    inv[:, half + 1:] = (-2.0 * np.sin(ang[1:])).T / length
    return split_bf16(fwd), split_bf16(inv)


def mm(a, b):
    return jnp.dot(a, b, preferred_element_type=F32)


def swap(x, bit):
    return lax.ppermute(x, "chan", [(c, c ^ bit) for c in range(4)])


def chan_sum(partial_out):
    core = lax.axis_index("chan") % 2
    width = partial_out.shape[1] // 2
    mine = lax.dynamic_slice_in_dim(partial_out, core * width, width, 1)
    other = lax.dynamic_slice_in_dim(partial_out, (1 - core) * width, width, 1)
    chip = mine + swap(other.astype(BF16), 1).astype(F32)
    total = (chip + swap(chip.astype(BF16), 2).astype(F32)).astype(BF16)
    peer = swap(total, 1)
    return jnp.where(core == 0, jnp.concatenate([total, peer], 1), jnp.concatenate([peer, total], 1))


def make_local(nseq, nchan):
    def local(value, first_gate, second_gate, first_filter, second_filter, out_weight, segment_ids):
        chans = value.shape[1]
        filt_local, length = first_filter.shape
        group = chans // filt_local
        per = chans // nseq
        fpd = per // group
        half = length // 2
        (f_hi, f_lo), (i_hi, i_lo) = dft_mats(length)
        f_hi, f_lo, i_hi, i_lo = (jnp.asarray(m) for m in (f_hi, f_lo, i_hi, i_lo))
        me = lax.axis_index("seq")


        def spectrum(filt):
            mine = lax.dynamic_slice_in_dim(filt, me * fpd, fpd, 0)
            taps = jnp.repeat(mine.T, group, axis=1)
            spec = mm(f_hi, taps) + mm(f_lo, taps)
            re, im = spec[:half], spec[half:]
            row0 = lax.broadcasted_iota(jnp.int32, re.shape, 0) == 0
            a = re
            b = jnp.where(row0, 0.0, im)
            d = jnp.where(row0, im, re)
            two = lambda x: jnp.concatenate([x, x], axis=1)
            return two(a), two(b), two(d)

        def long_conv(spec, field):
            a, b, d = spec
            zero = jnp.zeros_like(field)
            masked = jnp.concatenate(
                [jnp.where(in0, field, zero), jnp.where(in1, field, zero)], axis=1
            )
            x = mm(f_hi, masked) + mm(f_lo, masked)
            xr, xi = x[:half], x[half:]
            y = jnp.concatenate([xr * a - xi * b, xr * b + xi * d], axis=0)
            y_hi32 = lax.reduce_precision(y, exponent_bits=8, mantissa_bits=7)
            y_hi = y_hi32.astype(BF16)
            y_lo = (y - y_hi32).astype(BF16)
            both = mm(i_hi, y_hi) + mm(i_hi, y_lo) + mm(i_lo, y_hi)
            return jnp.where(in0, both[:, :per], 0.0) + jnp.where(in1, both[:, per:], 0.0)

        rows = value.shape[0]
        first_input = (first_gate.astype(F32) * value.astype(F32)).astype(BF16)
        id_rows = -(-rows // per)
        ids = jnp.pad(segment_ids.astype(BF16), (0, id_rows * per - rows)).reshape(id_rows, 1, per)
        ids = jnp.broadcast_to(ids, (id_rows, nseq, per))
        pad_rows = -(-id_rows // 16) * 16
        ids = jnp.pad(ids, ((0, pad_rows - id_rows), (0, 0), (0, 0)))
        payload = jnp.concatenate([first_input.reshape(rows, nseq, per), ids], axis=0)
        got = lax.all_to_all(payload.reshape(rows + pad_rows, nseq * per), "seq", 1, 0, tiled=True)
        got = got.reshape(nseq, rows + pad_rows, per)
        first_cols = got[:, :rows].reshape(nseq * rows, per)
        segs = got[:, rows:rows + id_rows].reshape(nseq, id_rows * per)[:, :rows].reshape(nseq * rows)
        in0 = (segs == 0)[:, None]
        in1 = (segs == 1)[:, None]
        gate_cols = lax.all_to_all(second_gate, "seq", 1, 0, tiled=True)
        first_mix = long_conv(spectrum(first_filter), first_cols)
        second_input = (gate_cols.astype(F32) * first_mix).astype(BF16)
        second_mix = long_conv(spectrum(second_filter), second_input).astype(BF16)
        mix_rows = lax.all_to_all(second_mix, "seq", 0, 1, tiled=True)
        partial_out = mm(mix_rows, out_weight)
        if nchan != 4:
            return lax.psum(partial_out, "chan").astype(BF16)
        return chan_sum(partial_out)

    return local


def solution(mesh):
    in_specs = (
        P(("groups", "seq"), "chan"),
        P(("groups", "seq"), "chan"),
        P(("groups", "seq"), "chan"),
        P("chan", None),
        P("chan", None),
        P("chan", None),
        P(("groups", "seq")),
    )
    out_specs = P(("groups", "seq"), None)
    local = make_local(mesh.shape["seq"], mesh.shape["chan"])
    return jax.shard_map(local, mesh=mesh, in_specs=in_specs, out_specs=out_specs, check_vma=False)
```

```python
import numpy as np
import jax
import jax.numpy as jnp
from jax import lax
from jax.sharding import PartitionSpec as P

F32 = jnp.float32
BF16 = jnp.bfloat16


def split_bf16(mat):
    hi = mat.astype(jnp.bfloat16)
    lo = (mat - hi.astype(np.float64)).astype(jnp.bfloat16)
    return hi, lo


def dft_mats(length):
    half = length // 2
    n = np.arange(length)
    f = np.arange(half)
    ang = 2.0 * np.pi * ((f[:, None] * n[None, :]) % length) / length
    fwd = np.zeros((length, length))
    fwd[:half] = np.cos(ang)
    fwd[half] = np.where(n % 2 == 0, 1.0, -1.0)
    fwd[half + 1:] = -np.sin(ang[1:])
    return split_bf16(fwd)


def mm(a, b):
    return jnp.dot(a, b, preferred_element_type=F32)


def swap(x, bit):
    return lax.ppermute(x, "chan", [(c, c ^ bit) for c in range(4)])


def chan_sum(partial_out):
    core = lax.axis_index("chan") % 2
    width = partial_out.shape[1] // 2
    mine = lax.dynamic_slice_in_dim(partial_out, core * width, width, 1)
    other = lax.dynamic_slice_in_dim(partial_out, (1 - core) * width, width, 1)
    chip = mine + swap(other.astype(BF16), 1).astype(F32)
    total = (chip + swap(chip.astype(BF16), 2).astype(F32)).astype(BF16)
    peer = swap(total, 1)
    return jnp.where(core == 0, jnp.concatenate([total, peer], 1), jnp.concatenate([peer, total], 1))


def make_local(nseq, nchan):
    def local(value, first_gate, second_gate, first_filter, second_filter, out_weight, segment_ids):
        rows, chans = value.shape
        filt_local, length = first_filter.shape
        group = chans // filt_local
        per = chans // nseq
        fpd = per // group
        half = length // 2
        f_hi, f_lo = dft_mats(length)
        f_blocks = np.stack(
            [np.concatenate([f_hi[:, b * rows:(b + 1) * rows], f_lo[:, b * rows:(b + 1) * rows]], axis=1)
             for b in range(nseq)]
        )
        f_blocks = jnp.asarray(f_blocks)
        me = lax.axis_index("seq")
        srcs = [(me - k) % nseq for k in range(nseq)]

        def shift(x, k):
            return lax.ppermute(x, "seq", [(i, (i + k) % nseq) for i in range(nseq)])

        def scatter_cols(x):
            out = [lax.dynamic_index_in_dim(x, me, 0, keepdims=False)]
            for k in range(1, nseq):
                out.append(shift(lax.dynamic_index_in_dim(x, (me + k) % nseq, 0, keepdims=False), k))
            return out

        def spectrum(filt):
            mine = lax.dynamic_slice_in_dim(filt, me * fpd, fpd, 0)
            taps = jnp.repeat(mine.T, group, axis=1)
            spec = None
            for b in range(nseq):
                blk = taps[b * rows:(b + 1) * rows]
                term = mm(f_blocks[b], jnp.concatenate([blk, blk], axis=0))
                spec = term if spec is None else spec + term
            re, im = spec[:half], spec[half:]
            row0 = lax.broadcasted_iota(jnp.int32, re.shape, 0) == 0
            two = lambda x: jnp.concatenate([x, x], axis=1)
            return two(re), two(jnp.where(row0, 0.0, im)), two(jnp.where(row0, im, re))

        def forward(pieces, piece_segs):
            x = None
            for k in range(nseq):
                z, sg = pieces[k], piece_segs[k][:, None]
                zero = jnp.zeros_like(z)
                masked = jnp.concatenate([jnp.where(sg == 0, z, zero), jnp.where(sg == 1, z, zero)], axis=1)
                term = mm(lax.dynamic_index_in_dim(f_blocks, srcs[k], 0, keepdims=False),
                          jnp.concatenate([masked, masked], axis=0))
                x = term if x is None else x + term
            return x

        weight = np.full((length, 1), 2.0 / length, np.float32)
        weight[0] = weight[half] = 1.0 / length
        weight = jnp.asarray(weight)

        def multiply(spec, x):
            a, b, d = spec
            xr, xi = x[:half], x[half:]
            y = jnp.concatenate([xr * a - xi * b, xr * b + xi * d], axis=0) * weight
            y_hi32 = lax.reduce_precision(y, exponent_bits=8, mantissa_bits=7)
            return y_hi32.astype(BF16), (y - y_hi32).astype(BF16)

        def mm_t(a, b):
            return lax.dot_general(a, b, (((0,), (0,)), ((), ())), preferred_element_type=F32)

        def inverse_block(y, dest):
            y_hi, y_lo = y
            blk = lax.dynamic_index_in_dim(f_blocks, dest, 0, keepdims=False)
            inv_hi, inv_lo = blk[:, :rows], blk[:, rows:]
            both = mm_t(inv_hi, y_hi) + mm_t(inv_hi, y_lo) + mm_t(inv_lo, y_hi)
            m0 = lax.dynamic_slice_in_dim(in0, dest * rows, rows, 0)
            m1 = lax.dynamic_slice_in_dim(in1, dest * rows, rows, 0)
            return jnp.where(m0, both[:, :per], 0.0) + jnp.where(m1, both[:, per:], 0.0)

        first_input = (first_gate.astype(F32) * value.astype(F32)).astype(BF16)
        first_input = first_input.reshape(rows, nseq, per).transpose(1, 0, 2)
        id_rows = -(-rows // per)
        pad_rows = -(-id_rows // 16) * 16
        ids = jnp.pad(segment_ids.astype(BF16), (0, pad_rows * per - rows)).reshape(1, pad_rows, per)
        payload = jnp.concatenate([first_input, jnp.broadcast_to(ids, (nseq, pad_rows, per))], axis=1)
        got = scatter_cols(payload)
        pieces1 = [g[:rows] for g in got]
        piece_segs = [g[rows:].reshape(pad_rows * per)[:rows] for g in got]
        gate_pieces = scatter_cols(second_gate.reshape(rows, nseq, per).transpose(1, 0, 2))

        by_shift = jnp.stack(piece_segs[::-1])
        segs = jnp.roll(by_shift, me + 1, axis=0).reshape(nseq * rows)
        in0 = (segs == 0)[:, None]
        in1 = (segs == 1)[:, None]

        spec1 = spectrum(first_filter)
        spec2 = spectrum(second_filter)
        y1 = multiply(spec1, forward(pieces1, piece_segs))
        first_mix = jnp.concatenate([inverse_block(y1, b) for b in range(nseq)], axis=0)

        pieces2 = []
        for k in range(nseq):
            fm = lax.dynamic_slice_in_dim(first_mix, srcs[k] * rows, rows, 0)
            pieces2.append((gate_pieces[k].astype(F32) * fm).astype(BF16))
        y2 = multiply(spec2, forward(pieces2, piece_segs))

        def out_block(dest):
            return inverse_block(y2, dest).astype(BF16)

        mix_pieces = [out_block(me)]
        for k in range(1, nseq):
            mix_pieces.append(shift(out_block((me + k) % nseq), k))

        def project(cols_lo, width):
            acc = None
            for k in range(nseq):
                w = lax.dynamic_slice(out_weight, (srcs[k] * per, cols_lo), (per, width))
                term = mm(mix_pieces[k], w)
                acc = term if acc is None else acc + term
            return acc

        if nchan != 4:
            return lax.psum(project(0, out_weight.shape[1]), "chan").astype(BF16)
        core = lax.axis_index("chan") % 2
        width = out_weight.shape[1] // 2
        other = project((1 - core) * width, width)
        got_other = swap(other.astype(BF16), 1)
        chip = project(core * width, width) + got_other.astype(F32)
        total = (chip + swap(chip.astype(BF16), 2).astype(F32)).astype(BF16)
        peer = swap(total, 1)
        return jnp.where(core == 0, jnp.concatenate([total, peer], 1), jnp.concatenate([peer, total], 1))

    return local


def solution(mesh):
    in_specs = (
        P(("groups", "seq"), "chan"),
        P(("groups", "seq"), "chan"),
        P(("groups", "seq"), "chan"),
        P("chan", None),
        P("chan", None),
        P("chan", None),
        P(("groups", "seq")),
    )
    out_specs = P(("groups", "seq"), None)
    local = make_local(mesh.shape["seq"], mesh.shape["chan"])
    return jax.shard_map(local, mesh=mesh, in_specs=in_specs, out_specs=out_specs, check_vma=False)
```

```python
import numpy as np
import jax
import jax.numpy as jnp
from jax import lax
from jax.sharding import PartitionSpec as P

F32 = jnp.float32
BF16 = jnp.bfloat16


def split_bf16(mat):
    hi = mat.astype(jnp.bfloat16)
    lo = (mat - hi.astype(np.float64)).astype(jnp.bfloat16)
    return hi, lo


def dft_mats(length):
    half = length // 2
    n = np.arange(length)
    f = np.arange(half)
    ang = 2.0 * np.pi * ((f[:, None] * n[None, :]) % length) / length
    fwd = np.zeros((length, length))
    fwd[:half] = np.cos(ang)
    fwd[half] = np.where(n % 2 == 0, 1.0, -1.0)
    fwd[half + 1:] = -np.sin(ang[1:])
    inv = np.zeros((length, length))
    scale = np.full(half, 2.0)
    scale[0] = 1.0
    inv[:, :half] = (np.cos(ang) * scale[:, None]).T / length
    inv[:, half] = np.where(n % 2 == 0, 1.0, -1.0) / length
    inv[:, half + 1:] = (-2.0 * np.sin(ang[1:])).T / length
    return split_bf16(fwd), split_bf16(inv)


def mm(a, b):
    return jnp.dot(a, b, preferred_element_type=F32)


def swap(x, bit):
    return lax.ppermute(x, "chan", [(c, c ^ bit) for c in range(4)])


def make_local(nseq, nchan):
    def local(value, first_gate, second_gate, first_filter, second_filter, out_weight, segment_ids):
        chans = value.shape[1]
        filt_local, length = first_filter.shape
        group = chans // filt_local
        per = chans // nseq
        fpd = per // group
        half = length // 2
        (f_hi, f_lo), (i_hi, i_lo) = dft_mats(length)
        f_hi, f_lo, i_hi, i_lo = (jnp.asarray(m) for m in (f_hi, f_lo, i_hi, i_lo))
        me = lax.axis_index("seq")


        def spectrum(filt):
            mine = lax.dynamic_slice_in_dim(filt, me * fpd, fpd, 0)
            taps = jnp.repeat(mine.T, group, axis=1)
            spec = mm(f_hi, taps) + mm(f_lo, taps)
            re, im = spec[:half], spec[half:]
            row0 = lax.broadcasted_iota(jnp.int32, re.shape, 0) == 0
            a = re
            b = jnp.where(row0, 0.0, im)
            d = jnp.where(row0, im, re)
            two = lambda x: jnp.concatenate([x, x], axis=1)
            return two(a), two(b), two(d)

        def long_conv(spec, field):
            a, b, d = spec
            zero = jnp.zeros_like(field)
            masked = jnp.concatenate(
                [jnp.where(in0, field, zero), jnp.where(in1, field, zero)], axis=1
            )
            x = mm(f_hi, masked) + mm(f_lo, masked)
            xr, xi = x[:half], x[half:]
            y = jnp.concatenate([xr * a - xi * b, xr * b + xi * d], axis=0)
            y_hi32 = lax.reduce_precision(y, exponent_bits=8, mantissa_bits=7)
            y_hi = y_hi32.astype(BF16)
            y_lo = (y - y_hi32).astype(BF16)
            both = mm(i_hi, y_hi) + mm(i_hi, y_lo) + mm(i_lo, y_hi)
            return jnp.where(in0, both[:, :per], 0.0) + jnp.where(in1, both[:, per:], 0.0)

        rows = value.shape[0]
        first_input = (first_gate.astype(F32) * value.astype(F32)).astype(BF16)
        first_input = first_input.reshape(rows, nseq, per).transpose(1, 0, 2)
        id_rows = -(-rows // per)
        pad_rows = -(-id_rows // 16) * 16
        ids = jnp.pad(segment_ids.astype(BF16), (0, pad_rows * per - rows)).reshape(1, pad_rows, per)
        payload = jnp.concatenate([first_input, jnp.broadcast_to(ids, (nseq, pad_rows, per))], axis=1)
        got = lax.all_to_all(payload, "seq", 0, 0, tiled=True)
        first_cols = got[:, :rows].reshape(nseq * rows, per)
        segs = got[:, rows:].reshape(nseq, pad_rows * per)[:, :rows].reshape(nseq * rows)
        in0 = (segs == 0)[:, None]
        in1 = (segs == 1)[:, None]
        gate_blocks = second_gate.reshape(rows, nseq, per).transpose(1, 0, 2)
        gate_cols = lax.all_to_all(gate_blocks, "seq", 0, 0, tiled=True).reshape(nseq * rows, per)
        first_mix = long_conv(spectrum(first_filter), first_cols)
        second_input = (gate_cols.astype(F32) * first_mix).astype(BF16)
        second_mix = long_conv(spectrum(second_filter), second_input).astype(BF16)
        mix_blocks = lax.all_to_all(second_mix.reshape(nseq, rows, per), "seq", 0, 0, tiled=True)
        out_cols = out_weight.shape[1]
        w_blocks = out_weight.reshape(nseq, per, out_cols)

        def project(w):
            return lax.dot_general(mix_blocks, w, (((0, 2), (0, 1)), ((), ())), preferred_element_type=F32)

        if nchan != 4:
            return lax.psum(project(w_blocks), "chan").astype(BF16)
        core = lax.axis_index("chan") % 2
        width = out_cols // 2
        w_halves = w_blocks.reshape(nseq, per, 2, width)
        other = project(lax.dynamic_index_in_dim(w_halves, 1 - core, 2, keepdims=False))
        got_other = swap(other.astype(BF16), 1)
        mine = project(lax.dynamic_index_in_dim(w_halves, core, 2, keepdims=False))
        chip = mine + got_other.astype(F32)
        total = (chip + swap(chip.astype(BF16), 2).astype(F32)).astype(BF16)
        peer = swap(total, 1)
        return jnp.where(core == 0, jnp.concatenate([total, peer], 1), jnp.concatenate([peer, total], 1))

    return local


def solution(mesh):
    in_specs = (
        P(("groups", "seq"), "chan"),
        P(("groups", "seq"), "chan"),
        P(("groups", "seq"), "chan"),
        P("chan", None),
        P("chan", None),
        P("chan", None),
        P(("groups", "seq")),
    )
    out_specs = P(("groups", "seq"), None)
    local = make_local(mesh.shape["seq"], mesh.shape["chan"])
    return jax.shard_map(local, mesh=mesh, in_specs=in_specs, out_specs=out_specs, check_vma=False)
```

```python
import numpy as np
import jax
import jax.numpy as jnp
from jax import lax
from jax.sharding import PartitionSpec as P

F32 = jnp.float32
BF16 = jnp.bfloat16


def split_bf16(mat):
    hi = mat.astype(jnp.bfloat16)
    lo = (mat - hi.astype(np.float64)).astype(jnp.bfloat16)
    return hi, lo


def dft_mats(length):
    half = length // 2
    n = np.arange(length)
    f = np.arange(half)
    ang = 2.0 * np.pi * ((f[:, None] * n[None, :]) % length) / length
    fwd = np.zeros((length, length))
    fwd[:half] = np.cos(ang)
    fwd[half] = np.where(n % 2 == 0, 1.0, -1.0)
    fwd[half + 1:] = -np.sin(ang[1:])
    inv = np.zeros((length, length))
    scale = np.full(half, 2.0)
    scale[0] = 1.0
    inv[:, :half] = (np.cos(ang) * scale[:, None]).T / length
    inv[:, half] = np.where(n % 2 == 0, 1.0, -1.0) / length
    inv[:, half + 1:] = (-2.0 * np.sin(ang[1:])).T / length
    return split_bf16(fwd), split_bf16(inv)


def mm(a, b):
    return jnp.dot(a, b, preferred_element_type=F32)


def swap(x, bit):
    return lax.ppermute(x, "chan", [(c, c ^ bit) for c in range(4)])


def make_local(nseq, nchan):
    def local(value, first_gate, second_gate, first_filter, second_filter, out_weight, segment_ids):
        chans = value.shape[1]
        filt_local, length = first_filter.shape
        group = chans // filt_local
        per = chans // nseq
        fpd = per // group
        half = length // 2
        (f_hi, f_lo), (i_hi, i_lo) = dft_mats(length)
        f_hi, f_lo, i_hi, i_lo = (jnp.asarray(m) for m in (f_hi, f_lo, i_hi, i_lo))
        me = lax.axis_index("seq")


        def spectrum(filt):
            mine = lax.dynamic_slice_in_dim(filt, me * fpd, fpd, 0)
            taps = jnp.repeat(mine.T, group, axis=1)
            spec = mm(f_hi, taps) + mm(f_lo, taps)
            re, im = spec[:half], spec[half:]
            row0 = lax.broadcasted_iota(jnp.int32, re.shape, 0) == 0
            a = re
            b = jnp.where(row0, 0.0, im)
            d = jnp.where(row0, im, re)
            two = lambda x: jnp.concatenate([x, x], axis=1)
            return two(a), two(b), two(d)

        def long_conv(spec, field):
            a, b, d = spec
            zero = jnp.zeros_like(field)
            masked = jnp.concatenate(
                [jnp.where(in0, field, zero), jnp.where(in1, field, zero)], axis=1
            )
            x = mm(f_hi, masked) + mm(f_lo, masked)
            xr, xi = x[:half], x[half:]
            y = jnp.concatenate([xr * a - xi * b, xr * b + xi * d], axis=0)
            y_hi32 = lax.reduce_precision(y, exponent_bits=8, mantissa_bits=7)
            y_hi = y_hi32.astype(BF16)
            y_lo = (y - y_hi32).astype(BF16)
            both = mm(i_hi, y_hi) + mm(i_hi, y_lo) + mm(i_lo, y_hi)
            return jnp.where(in0, both[:, :per], 0.0) + jnp.where(in1, both[:, per:], 0.0)

        rows = value.shape[0]
        first_input = (first_gate.astype(F32) * value.astype(F32)).astype(BF16)
        first_input = first_input.reshape(rows, nseq, per).transpose(1, 0, 2)
        id_rows = -(-rows // per)
        pad_rows = -(-id_rows // 16) * 16
        ids = jnp.pad(segment_ids.astype(BF16), (0, pad_rows * per - rows)).reshape(1, pad_rows, per)
        payload = jnp.concatenate([first_input, jnp.broadcast_to(ids, (nseq, pad_rows, per))], axis=1)
        got = lax.all_to_all(payload, "seq", 0, 0, tiled=True)
        first_cols = got[:, :rows].reshape(nseq * rows, per)
        segs = got[:, rows:].reshape(nseq, pad_rows * per)[:, :rows].reshape(nseq * rows)
        in0 = (segs == 0)[:, None]
        in1 = (segs == 1)[:, None]
        gate_blocks = second_gate.reshape(rows, nseq, per).transpose(1, 0, 2)
        gate_cols = lax.all_to_all(gate_blocks, "seq", 0, 0, tiled=True).reshape(nseq * rows, per)
        first_mix = long_conv(spectrum(first_filter), first_cols)
        second_input = (gate_cols.astype(F32) * first_mix).astype(BF16)
        second_mix = long_conv(spectrum(second_filter), second_input).astype(BF16)
        mix_blocks = lax.all_to_all(second_mix.reshape(nseq, rows, per), "seq", 0, 0, tiled=True)
        out_cols = out_weight.shape[1]
        mix_rows = mix_blocks.transpose(1, 0, 2).reshape(rows, nseq * per)

        def project(w):
            return mm(mix_rows, w)

        if nchan != 4:
            return lax.psum(project(out_weight), "chan").astype(BF16)
        core = lax.axis_index("chan") % 2
        width = out_cols // 2
        other = project(lax.dynamic_slice_in_dim(out_weight, (1 - core) * width, width, 1))
        got_other = swap(other.astype(BF16), 1)
        mine = project(lax.dynamic_slice_in_dim(out_weight, core * width, width, 1))
        chip = mine + got_other.astype(F32)
        total = (chip + swap(chip.astype(BF16), 2).astype(F32)).astype(BF16)
        peer = swap(total, 1)
        return jnp.where(core == 0, jnp.concatenate([total, peer], 1), jnp.concatenate([peer, total], 1))

    return local


def solution(mesh):
    in_specs = (
        P(("groups", "seq"), "chan"),
        P(("groups", "seq"), "chan"),
        P(("groups", "seq"), "chan"),
        P("chan", None),
        P("chan", None),
        P("chan", None),
        P(("groups", "seq")),
    )
    out_specs = P(("groups", "seq"), None)
    local = make_local(mesh.shape["seq"], mesh.shape["chan"])
    return jax.shard_map(local, mesh=mesh, in_specs=in_specs, out_specs=out_specs, check_vma=False)
```

```python
import numpy as np
import jax
import jax.numpy as jnp
from jax import lax
from jax.sharding import PartitionSpec as P

F32 = jnp.float32
BF16 = jnp.bfloat16


def split_bf16(mat):
    hi = mat.astype(jnp.bfloat16)
    lo = (mat - hi.astype(np.float64)).astype(jnp.bfloat16)
    return hi, lo


def dft_mats(length):
    half = length // 2
    n = np.arange(length)
    f = np.arange(half)
    ang = 2.0 * np.pi * ((f[:, None] * n[None, :]) % length) / length
    fwd = np.zeros((length, length))
    fwd[:half] = np.cos(ang)
    fwd[half] = np.where(n % 2 == 0, 1.0, -1.0)
    fwd[half + 1:] = -np.sin(ang[1:])
    inv = np.zeros((length, length))
    scale = np.full(half, 2.0)
    scale[0] = 1.0
    inv[:, :half] = (np.cos(ang) * scale[:, None]).T / length
    inv[:, half] = np.where(n % 2 == 0, 1.0, -1.0) / length
    inv[:, half + 1:] = (-2.0 * np.sin(ang[1:])).T / length
    return split_bf16(fwd), split_bf16(inv)


def mm(a, b):
    return jnp.dot(a, b, preferred_element_type=F32)


def swap(x, bit):
    return lax.ppermute(x, "chan", [(c, c ^ bit) for c in range(4)])


def make_local(nseq, nchan):
    def local(value, first_gate, second_gate, first_filter, second_filter, out_weight, segment_ids):
        chans = value.shape[1]
        filt_local, length = first_filter.shape
        group = chans // filt_local
        per = chans // nseq
        fpd = per // group
        half = length // 2
        (f_hi, f_lo), (i_hi, i_lo) = dft_mats(length)
        f_hi, f_lo, i_hi, i_lo = (jnp.asarray(m) for m in (f_hi, f_lo, i_hi, i_lo))

        def spectrum(filt):
            mine = lax.dynamic_slice_in_dim(filt, me * fpd, fpd, 0)
            taps = jnp.repeat(mine.T, group, axis=1)
            spec = mm(f_hi, taps) + mm(f_lo, taps)
            re, im = spec[:half], spec[half:]
            row0 = lax.broadcasted_iota(jnp.int32, re.shape, 0) == 0
            a = re
            b = jnp.where(row0, 0.0, im)
            d = jnp.where(row0, im, re)
            two = lambda x: jnp.concatenate([x, x], axis=1)
            return two(a), two(b), two(d)

        def long_conv(spec, field):
            a, b, d = spec
            zero = jnp.zeros_like(field)
            masked = jnp.concatenate(
                [jnp.where(in0, field, zero), jnp.where(in1, field, zero)], axis=1
            )
            x = mm(f_hi, masked) + mm(f_lo, masked)
            xr, xi = x[:half], x[half:]
            y = jnp.concatenate([xr * a - xi * b, xr * b + xi * d], axis=0)
            y_hi32 = lax.reduce_precision(y, exponent_bits=8, mantissa_bits=7)
            y_hi = y_hi32.astype(BF16)
            y_lo = (y - y_hi32).astype(BF16)
            both = mm(i_hi, y_hi) + mm(i_hi, y_lo) + mm(i_lo, y_hi)
            return jnp.where(in0, both[:, :per], 0.0) + jnp.where(in1, both[:, per:], 0.0)

        rows = value.shape[0]
        me = lax.axis_index("seq")
        order = [0] + [k for k in (1, nseq - 1) if k < nseq] + [k for k in range(2, nseq - 1)]
        order = list(dict.fromkeys(order))

        def exchange(blocks):
            got = {0: lax.dynamic_index_in_dim(blocks, me, 0, keepdims=False)}
            for k in order[1:]:
                piece = lax.dynamic_index_in_dim(blocks, (me + k) % nseq, 0, keepdims=False)
                got[k] = lax.ppermute(piece, "seq", [(i, (i + k) % nseq) for i in range(nseq)])
            return got

        def in_source_order(got):
            by_shift = jnp.stack([got[k] for k in reversed(range(nseq))])
            return jnp.roll(by_shift, me + 1, axis=0)

        first_input = (first_gate.astype(F32) * value.astype(F32)).astype(BF16)
        first_input = first_input.reshape(rows, nseq, per).transpose(1, 0, 2)
        gate_blocks = second_gate.reshape(rows, nseq, per).transpose(1, 0, 2)
        id_rows = -(-rows // per)
        pad_rows = -(-id_rows // 16) * 16
        ids = jnp.pad(segment_ids.astype(BF16), (0, pad_rows * per - rows)).reshape(1, pad_rows, per)
        payload = jnp.concatenate(
            [first_input, gate_blocks, jnp.broadcast_to(ids, (nseq, pad_rows, per))], axis=1)
        got = in_source_order(exchange(payload))
        first_cols = got[:, :rows].reshape(nseq * rows, per)
        gate_cols = got[:, rows:2 * rows].reshape(nseq * rows, per)
        segs = got[:, 2 * rows:].reshape(nseq, pad_rows * per)[:, :rows].reshape(nseq * rows)
        in0 = (segs == 0)[:, None]
        in1 = (segs == 1)[:, None]
        first_mix = long_conv(spectrum(first_filter), first_cols)
        second_input = (gate_cols.astype(F32) * first_mix).astype(BF16)
        second_mix = long_conv(spectrum(second_filter), second_input).astype(BF16)
        mix_pieces = exchange(second_mix.reshape(nseq, rows, per))
        out_cols = out_weight.shape[1]

        def project(cols_lo, width):
            acc = None
            for k in order:
                w = lax.dynamic_slice(out_weight, (((me - k) % nseq) * per, cols_lo), (per, width))
                term = mm(mix_pieces[k], w)
                acc = term if acc is None else acc + term
            return acc

        if nchan != 4:
            return lax.psum(project(0, out_cols), "chan").astype(BF16)
        core = lax.axis_index("chan") % 2
        width = out_cols // 2
        other = project((1 - core) * width, width)
        got_other = swap(other.astype(BF16), 1)
        mine = project(core * width, width)
        chip = mine + got_other.astype(F32)
        total = (chip + swap(chip.astype(BF16), 2).astype(F32)).astype(BF16)
        peer = swap(total, 1)
        return jnp.where(core == 0, jnp.concatenate([total, peer], 1), jnp.concatenate([peer, total], 1))

    return local


def solution(mesh):
    in_specs = (
        P(("groups", "seq"), "chan"),
        P(("groups", "seq"), "chan"),
        P(("groups", "seq"), "chan"),
        P("chan", None),
        P("chan", None),
        P("chan", None),
        P(("groups", "seq")),
    )
    out_specs = P(("groups", "seq"), None)
    local = make_local(mesh.shape["seq"], mesh.shape["chan"])
    return jax.shard_map(local, mesh=mesh, in_specs=in_specs, out_specs=out_specs, check_vma=False)
```

```python
import numpy as np
import jax
import jax.numpy as jnp
from jax import lax
from jax.sharding import PartitionSpec as P

F32 = jnp.float32
BF16 = jnp.bfloat16


def split_bf16(mat):
    hi = mat.astype(jnp.bfloat16)
    lo = (mat - hi.astype(np.float64)).astype(jnp.bfloat16)
    return hi, lo


def dft_mats(length):
    half = length // 2
    n = np.arange(length)
    f = np.arange(half)
    ang = 2.0 * np.pi * ((f[:, None] * n[None, :]) % length) / length
    fwd = np.zeros((length, length))
    fwd[:half] = np.cos(ang)
    fwd[half] = np.where(n % 2 == 0, 1.0, -1.0)
    fwd[half + 1:] = -np.sin(ang[1:])
    inv = np.zeros((length, length))
    scale = np.full(half, 2.0)
    scale[0] = 1.0
    inv[:, :half] = (np.cos(ang) * scale[:, None]).T / length
    inv[:, half] = np.where(n % 2 == 0, 1.0, -1.0) / length
    inv[:, half + 1:] = (-2.0 * np.sin(ang[1:])).T / length
    return split_bf16(fwd), split_bf16(inv)


def mm(a, b):
    return jnp.dot(a, b, preferred_element_type=F32)


def swap(x, bit):
    return lax.ppermute(x, "chan", [(c, c ^ bit) for c in range(4)])


def make_local(nseq, nchan):
    def local(value, first_gate, second_gate, first_filter, second_filter, out_weight, segment_ids):
        chans = value.shape[1]
        filt_local, length = first_filter.shape
        group = chans // filt_local
        per = chans // nseq
        fpd = per // group
        half = length // 2
        (f_hi, f_lo), (i_hi, i_lo) = dft_mats(length)
        f_hi, f_lo, i_hi, i_lo = (jnp.asarray(m) for m in (f_hi, f_lo, i_hi, i_lo))

        def spectrum(filt):
            mine = lax.dynamic_slice_in_dim(filt, me * fpd, fpd, 0)
            taps = jnp.repeat(mine.T, group, axis=1)
            spec = mm(f_hi, taps) + mm(f_lo, taps)
            re, im = spec[:half], spec[half:]
            row0 = lax.broadcasted_iota(jnp.int32, re.shape, 0) == 0
            a = re
            b = jnp.where(row0, 0.0, im)
            d = jnp.where(row0, im, re)
            two = lambda x: jnp.concatenate([x, x], axis=1)
            return two(a), two(b), two(d)

        def long_conv(spec, field):
            a, b, d = spec
            zero = jnp.zeros_like(field)
            masked = jnp.concatenate(
                [jnp.where(in0, field, zero), jnp.where(in1, field, zero)], axis=1
            )
            x = mm(f_hi, masked) + mm(f_lo, masked)
            xr, xi = x[:half], x[half:]
            y = jnp.concatenate([xr * a - xi * b, xr * b + xi * d], axis=0)
            y_hi32 = lax.reduce_precision(y, exponent_bits=8, mantissa_bits=7)
            y_hi = y_hi32.astype(BF16)
            y_lo = (y - y_hi32).astype(BF16)
            both = mm(i_hi, y_hi) + mm(i_hi, y_lo) + mm(i_lo, y_hi)
            return jnp.where(in0, both[:, :per], 0.0) + jnp.where(in1, both[:, per:], 0.0)

        rows = value.shape[0]
        me = lax.axis_index("seq")
        order = [0] + [k for k in (1, nseq - 1) if k < nseq] + [k for k in range(2, nseq - 1)]
        order = list(dict.fromkeys(order))

        def rotated(got):
            return jnp.concatenate([got[(nseq - j) % nseq] for j in range(nseq)], axis=0)

        first_input = (first_gate.astype(F32) * value.astype(F32)).astype(BF16)
        id_rows = -(-rows // per)
        pad_rows = -(-id_rows // 16) * 16
        ids = jnp.pad(segment_ids.astype(BF16), (0, pad_rows * per - rows)).reshape(pad_rows, per)

        def block_for(dest):
            cols = lambda x: lax.dynamic_slice_in_dim(x, dest * per, per, 1)
            return jnp.concatenate([cols(first_input), cols(second_gate), ids], axis=0)

        got = {0: block_for(me)}
        for k in order[1:]:
            got[k] = lax.ppermute(block_for((me + k) % nseq), "seq", [(i, (i + k) % nseq) for i in range(nseq)])
        got = rotated(got).reshape(nseq, 2 * rows + pad_rows, per)
        first_cols = got[:, :rows].reshape(nseq * rows, per)
        gate_cols = got[:, rows:2 * rows].reshape(nseq * rows, per)
        segs = got[:, 2 * rows:].reshape(nseq, pad_rows * per)[:, :rows].reshape(nseq * rows)
        in0 = (segs == 0)[:, None]
        in1 = (segs == 1)[:, None]
        first_mix = long_conv(spectrum(first_filter), first_cols)
        second_input = (gate_cols.astype(F32) * first_mix).astype(BF16)
        second_mix = long_conv(spectrum(second_filter), second_input).astype(BF16)
        mix_pieces = {0: second_mix[:rows]}
        for k in order[1:]:
            mix_pieces[k] = lax.ppermute(second_mix[k * rows:(k + 1) * rows], "seq",
                                         [(i, (i + k) % nseq) for i in range(nseq)])
        out_cols = out_weight.shape[1]

        def project(cols_lo, width):
            acc = None
            for k in order:
                w = lax.dynamic_slice(out_weight, (((me - k) % nseq) * per, cols_lo), (per, width))
                term = mm(mix_pieces[k], w)
                acc = term if acc is None else acc + term
            return acc

        if nchan != 4:
            return lax.psum(project(0, out_cols), "chan").astype(BF16)
        core = lax.axis_index("chan") % 2
        width = out_cols // 2
        other = project((1 - core) * width, width)
        got_other = swap(other.astype(BF16), 1)
        mine = project(core * width, width)
        chip = mine + got_other.astype(F32)
        total = (chip + swap(chip.astype(BF16), 2).astype(F32)).astype(BF16)
        peer = swap(total, 1)
        return jnp.where(core == 0, jnp.concatenate([total, peer], 1), jnp.concatenate([peer, total], 1))

    return local


def solution(mesh):
    in_specs = (
        P(("groups", "seq"), "chan"),
        P(("groups", "seq"), "chan"),
        P(("groups", "seq"), "chan"),
        P("chan", None),
        P("chan", None),
        P("chan", None),
        P(("groups", "seq")),
    )
    out_specs = P(("groups", "seq"), None)
    local = make_local(mesh.shape["seq"], mesh.shape["chan"])
    return jax.shard_map(local, mesh=mesh, in_specs=in_specs, out_specs=out_specs, check_vma=False)
```

```python
import numpy as np
import jax
import jax.numpy as jnp
from jax import lax
from jax.sharding import PartitionSpec as P
from jax.experimental import pallas as pl
from jax.experimental.pallas import tpu as pltpu

F32 = jnp.float32
BF16 = jnp.bfloat16


def split_bf16(mat):
    hi = mat.astype(jnp.bfloat16)
    lo = (mat - hi.astype(np.float64)).astype(jnp.bfloat16)
    return hi, lo


def dft_mats(length):
    half = length // 2
    n = np.arange(length)
    f = np.arange(half)
    ang = 2.0 * np.pi * ((f[:, None] * n[None, :]) % length) / length
    fwd = np.zeros((length, length))
    fwd[:half] = np.cos(ang)
    fwd[half] = np.where(n % 2 == 0, 1.0, -1.0)
    fwd[half + 1:] = -np.sin(ang[1:])
    inv = np.zeros((length, length))
    scale = np.full(half, 2.0)
    scale[0] = 1.0
    inv[:, :half] = (np.cos(ang) * scale[:, None]).T / length
    inv[:, half] = np.where(n % 2 == 0, 1.0, -1.0) / length
    inv[:, half + 1:] = (-2.0 * np.sin(ang[1:])).T / length
    return split_bf16(fwd), split_bf16(inv)


def conv_kernel(z_ref, m0_ref, m1_ref, a_ref, b_ref, d_ref, fhi_ref, flo_ref, ihi_ref, ilo_ref, o_ref):
    length, per = z_ref.shape
    half = length // 2
    z = z_ref[...].astype(F32)
    m0 = m0_ref[...]
    m1 = m1_ref[...]
    masked = jnp.concatenate([z * m0, z * m1], axis=1).astype(BF16)
    x = (jnp.dot(fhi_ref[...], masked, preferred_element_type=F32)
         + jnp.dot(flo_ref[...], masked, preferred_element_type=F32))
    a = a_ref[...]
    b = b_ref[...]
    d = d_ref[...]
    a2 = jnp.concatenate([a, a], axis=1)
    b2 = jnp.concatenate([b, b], axis=1)
    d2 = jnp.concatenate([d, d], axis=1)
    xr = x[:half]
    xi = x[half:]
    y = jnp.concatenate([xr * a2 - xi * b2, xr * b2 + xi * d2], axis=0)
    y_hi = y.astype(BF16)
    y_lo = (y - y_hi.astype(F32)).astype(BF16)
    ihi = ihi_ref[...]
    both = (jnp.dot(ihi, y_hi, preferred_element_type=F32)
            + jnp.dot(ihi, y_lo, preferred_element_type=F32)
            + jnp.dot(ilo_ref[...], y_hi, preferred_element_type=F32))
    o_ref[...] = (both[:, :per] * m0 + both[:, per:] * m1).astype(o_ref.dtype)


def conv_call(field, m0, m1, spec, mats, out_dtype):
    length, per = field.shape
    flops = 2 * length * length * 2 * per * 5
    return pl.pallas_call(
        conv_kernel,
        out_shape=jax.ShapeDtypeStruct((length, per), out_dtype),
        compiler_params=pltpu.CompilerParams(vmem_limit_bytes=48 * 1024 * 1024),
        cost_estimate=pl.CostEstimate(flops=flops, transcendentals=0, bytes_accessed=4 * length * length * 2 + 6 * length * per),
    )(field, m0, m1, *spec, *mats)


def mm(a, b):
    return jnp.dot(a, b, preferred_element_type=F32)


def swap(x, bit):
    return lax.ppermute(x, "chan", [(c, c ^ bit) for c in range(4)])


def make_local(nseq, nchan):
    def local(value, first_gate, second_gate, first_filter, second_filter, out_weight, segment_ids):
        chans = value.shape[1]
        filt_local, length = first_filter.shape
        group = chans // filt_local
        per = chans // nseq
        fpd = per // group
        half = length // 2
        (f_hi, f_lo), (i_hi, i_lo) = dft_mats(length)
        f_hi, f_lo, i_hi, i_lo = (jnp.asarray(m) for m in (f_hi, f_lo, i_hi, i_lo))

        def spectrum(filt):
            mine = lax.dynamic_slice_in_dim(filt, me * fpd, fpd, 0)
            taps = jnp.repeat(mine.T, group, axis=1)
            spec = mm(f_hi, taps) + mm(f_lo, taps)
            re, im = spec[:half], spec[half:]
            row0 = lax.broadcasted_iota(jnp.int32, re.shape, 0) == 0
            a = re
            b = jnp.where(row0, 0.0, im)
            d = jnp.where(row0, im, re)
            return a, b, d

        def long_conv(spec, field, out_dtype=F32):
            return conv_call(field, in0, in1, spec, (f_hi, f_lo, i_hi, i_lo), out_dtype)

        rows = value.shape[0]
        me = lax.axis_index("seq")
        order = [0] + [k for k in (1, nseq - 1) if k < nseq] + [k for k in range(2, nseq - 1)]
        order = list(dict.fromkeys(order))

        def rotated(got):
            return jnp.concatenate([got[(nseq - j) % nseq] for j in range(nseq)], axis=0)

        first_input = (first_gate.astype(F32) * value.astype(F32)).astype(BF16)
        id_rows = -(-rows // per)
        pad_rows = -(-id_rows // 16) * 16
        ids = jnp.pad(segment_ids.astype(BF16), (0, pad_rows * per - rows)).reshape(pad_rows, per)

        def block_for(dest):
            cols = lambda x: lax.dynamic_slice_in_dim(x, dest * per, per, 1)
            return jnp.concatenate([cols(first_input), cols(second_gate), ids], axis=0)

        got = {0: block_for(me)}
        for k in order[1:]:
            got[k] = lax.ppermute(block_for((me + k) % nseq), "seq", [(i, (i + k) % nseq) for i in range(nseq)])
        got = rotated(got).reshape(nseq, 2 * rows + pad_rows, per)
        first_cols = got[:, :rows].reshape(nseq * rows, per)
        gate_cols = got[:, rows:2 * rows].reshape(nseq * rows, per)
        segs = got[:, 2 * rows:].reshape(nseq, pad_rows * per)[:, :rows].reshape(nseq * rows)
        in0 = (segs == 0).astype(F32)[:, None]
        in1 = (segs == 1).astype(F32)[:, None]
        first_mix = long_conv(spectrum(first_filter), first_cols)
        second_input = (gate_cols.astype(F32) * first_mix).astype(BF16)
        second_mix = long_conv(spectrum(second_filter), second_input, BF16)
        mix_pieces = {0: second_mix[:rows]}
        for k in order[1:]:
            mix_pieces[k] = lax.ppermute(second_mix[k * rows:(k + 1) * rows], "seq",
                                         [(i, (i + k) % nseq) for i in range(nseq)])
        out_cols = out_weight.shape[1]

        def project(cols_lo, width):
            acc = None
            for k in order:
                w = lax.dynamic_slice(out_weight, (((me - k) % nseq) * per, cols_lo), (per, width))
                term = mm(mix_pieces[k], w)
                acc = term if acc is None else acc + term
            return acc

        if nchan != 4:
            return lax.psum(project(0, out_cols), "chan").astype(BF16)
        core = lax.axis_index("chan") % 2
        width = out_cols // 2
        other = project((1 - core) * width, width)
        got_other = swap(other.astype(BF16), 1)
        mine = project(core * width, width)
        chip = mine + got_other.astype(F32)
        total = (chip + swap(chip.astype(BF16), 2).astype(F32)).astype(BF16)
        peer = swap(total, 1)
        return jnp.where(core == 0, jnp.concatenate([total, peer], 1), jnp.concatenate([peer, total], 1))

    return local


def solution(mesh):
    in_specs = (
        P(("groups", "seq"), "chan"),
        P(("groups", "seq"), "chan"),
        P(("groups", "seq"), "chan"),
        P("chan", None),
        P("chan", None),
        P("chan", None),
        P(("groups", "seq")),
    )
    out_specs = P(("groups", "seq"), None)
    local = make_local(mesh.shape["seq"], mesh.shape["chan"])
    return jax.shard_map(local, mesh=mesh, in_specs=in_specs, out_specs=out_specs, check_vma=False)
```

```python
import functools
import numpy as np
import jax
import jax.numpy as jnp
from jax import lax
from jax.sharding import PartitionSpec as P
from jax.experimental import pallas as pl
from jax.experimental.pallas import tpu as pltpu

F32 = jnp.float32
BF16 = jnp.bfloat16


def split_bf16(mat):
    hi = mat.astype(jnp.bfloat16)
    lo = (mat - hi.astype(np.float64)).astype(jnp.bfloat16)
    return hi, lo


def dft_mats(length):
    half = length // 2
    n = np.arange(length)
    f = np.arange(half)
    ang = 2.0 * np.pi * ((f[:, None] * n[None, :]) % length) / length
    fwd = np.zeros((length, length))
    fwd[:half] = np.cos(ang)
    fwd[half] = np.where(n % 2 == 0, 1.0, -1.0)
    fwd[half + 1:] = -np.sin(ang[1:])
    inv = np.zeros((length, length))
    scale = np.full(half, 2.0)
    scale[0] = 1.0
    inv[:, :half] = (np.cos(ang) * scale[:, None]).T / length
    inv[:, half] = np.where(n % 2 == 0, 1.0, -1.0) / length
    inv[:, half + 1:] = (-2.0 * np.sin(ang[1:])).T / length
    return split_bf16(fwd), split_bf16(inv)


def round_bf16(x, in_kernel):
    if in_kernel:
        return x.astype(BF16).astype(F32)
    return lax.reduce_precision(x, exponent_bits=8, mantissa_bits=7)


def hyena_math(pieces, m0, m1, spec1, spec2, mats, rows, wait, in_kernel):
    nseq = len(pieces)
    per = pieces[0].shape[1]
    length = m0.shape[0]
    half = length // 2
    order = [(nseq - j) % nseq for j in range(nseq)]
    first = jnp.concatenate([pieces[k][0:rows, :] for k in order], axis=0).astype(F32)
    gate = jnp.concatenate([pieces[k][rows:2 * rows, :] for k in order], axis=0).astype(F32)

    def conv(z, spec, first_call):
        masked = jnp.concatenate([z * m0, z * m1], axis=1).astype(BF16)
        if first_call:
            wait(0)
            wait(1)
        x = (jnp.dot(mats[0](), masked, preferred_element_type=F32)
             + jnp.dot(mats[1](), masked, preferred_element_type=F32))
        a, b, d = (jnp.concatenate([v, v], axis=1) for v in (f() for f in spec))
        xr = x[:half]
        xi = x[half:]
        y = jnp.concatenate([xr * a - xi * b, xr * b + xi * d], axis=0)
        y_hi32 = round_bf16(y, in_kernel)
        y_hi = y_hi32.astype(BF16)
        y_lo = (y - y_hi32).astype(BF16)
        if first_call:
            wait(2)
            wait(3)
        ihi = mats[2]()
        both = (jnp.dot(ihi, y_hi, preferred_element_type=F32)
                + jnp.dot(ihi, y_lo, preferred_element_type=F32)
                + jnp.dot(mats[3](), y_hi, preferred_element_type=F32))
        return both[:, :per] * m0 + both[:, per:] * m1

    first_mix = conv(first, spec1, True)
    second_input = round_bf16(gate * first_mix, in_kernel)
    return conv(second_input, spec2, False).astype(BF16)


def hyena_kernel(*refs, nseq, rows):
    pieces = [r[...] for r in refs[:nseq]]
    m0_ref, m1_ref = refs[nseq:nseq + 2]
    spec_refs = refs[nseq + 2:nseq + 8]
    mats_hbm = refs[nseq + 8:nseq + 12]
    o_ref = refs[nseq + 12]
    mats = refs[nseq + 13:nseq + 17]
    sem = refs[nseq + 17]
    copies = [pltpu.make_async_copy(mats_hbm[i], mats[i], sem.at[i]) for i in range(4)]
    for c in copies:
        c.start()
    loader = lambda r: (lambda: r[...])
    spec1 = [loader(r) for r in spec_refs[:3]]
    spec2 = [loader(r) for r in spec_refs[3:]]
    o_ref[...] = hyena_math(pieces, m0_ref[...], m1_ref[...], spec1, spec2,
                            [loader(r) for r in mats], rows, lambda i: copies[i].wait(), True)


def hyena_call(pieces, m0, m1, spec1, spec2, mats, rows):
    nseq = len(pieces)
    length = m0.shape[0]
    per = pieces[0].shape[1]
    if 4 * length * length * 2 > 8 * 1024 * 1024:
        const = lambda v: (lambda: v)
        return hyena_math(pieces, m0, m1, [const(v) for v in spec1], [const(v) for v in spec2],
                          [const(v) for v in mats], rows, lambda i: None, False)
    vmem = pl.BlockSpec(memory_space=pltpu.VMEM)
    hbm = pl.BlockSpec(memory_space=pl.ANY)
    flops = 2 * (2 * length * length * 2 * per * 5)
    return pl.pallas_call(
        functools.partial(hyena_kernel, nseq=nseq, rows=rows),
        out_shape=jax.ShapeDtypeStruct((length, per), BF16),
        in_specs=[vmem] * (nseq + 8) + [hbm] * 4,
        out_specs=vmem,
        scratch_shapes=[pltpu.VMEM((length, length), BF16) for _ in range(4)]
        + [pltpu.SemaphoreType.DMA((4,))],
        compiler_params=pltpu.CompilerParams(vmem_limit_bytes=56 * 1024 * 1024),
        cost_estimate=pl.CostEstimate(flops=flops, transcendentals=0,
                                      bytes_accessed=4 * length * length * 2 + 8 * length * per),
    )(*pieces, m0, m1, *spec1, *spec2, *mats)

def mm(a, b):
    return jnp.dot(a, b, preferred_element_type=F32)


def swap(x, bit):
    return lax.ppermute(x, "chan", [(c, c ^ bit) for c in range(4)])


def make_local(nseq, nchan):
    def local(value, first_gate, second_gate, first_filter, second_filter, out_weight, segment_ids):
        chans = value.shape[1]
        filt_local, length = first_filter.shape
        group = chans // filt_local
        per = chans // nseq
        fpd = per // group
        half = length // 2
        (f_hi, f_lo), (i_hi, i_lo) = dft_mats(length)
        f_hi, f_lo, i_hi, i_lo = (jnp.asarray(m) for m in (f_hi, f_lo, i_hi, i_lo))

        def spectrum(filt):
            mine = lax.dynamic_slice_in_dim(filt, me * fpd, fpd, 0)
            taps = jnp.repeat(mine.T, group, axis=1)
            spec = mm(f_hi, taps) + mm(f_lo, taps)
            re, im = spec[:half], spec[half:]
            row0 = lax.broadcasted_iota(jnp.int32, re.shape, 0) == 0
            a = re
            b = jnp.where(row0, 0.0, im)
            d = jnp.where(row0, im, re)
            return a, b, d

        rows = value.shape[0]
        me = lax.axis_index("seq")
        order = [0] + [k for k in (1, nseq - 1) if k < nseq] + [k for k in range(2, nseq - 1)]
        order = list(dict.fromkeys(order))

        first_input = (first_gate.astype(F32) * value.astype(F32)).astype(BF16)
        id_rows = -(-rows // per)
        pad_rows = -(-id_rows // 16) * 16
        ids = jnp.pad(segment_ids.astype(BF16), (0, pad_rows * per - rows)).reshape(pad_rows, per)

        def block_for(dest):
            cols = lambda x: lax.dynamic_slice_in_dim(x, dest * per, per, 1)
            return jnp.concatenate([cols(first_input), cols(second_gate), ids], axis=0)

        got = {0: block_for(me)}
        for k in order[1:]:
            got[k] = lax.ppermute(block_for((me + k) % nseq), "seq", [(i, (i + k) % nseq) for i in range(nseq)])
        seg_blocks = jnp.stack([got[(nseq - j) % nseq][2 * rows:] for j in range(nseq)])
        segs = seg_blocks.reshape(nseq, pad_rows * per)[:, :rows].reshape(nseq * rows)
        in0 = (segs == 0).astype(F32)[:, None]
        in1 = (segs == 1).astype(F32)[:, None]
        second_mix = hyena_call([got[k] for k in range(nseq)], in0, in1, spectrum(first_filter),
                                spectrum(second_filter), (f_hi, f_lo, i_hi, i_lo), rows)
        mix_pieces = {0: second_mix[:rows]}
        for k in order[1:]:
            mix_pieces[k] = lax.ppermute(second_mix[k * rows:(k + 1) * rows], "seq",
                                         [(i, (i + k) % nseq) for i in range(nseq)])
        out_cols = out_weight.shape[1]

        def project(cols_lo, width):
            acc = None
            for k in order:
                w = lax.dynamic_slice(out_weight, (((me - k) % nseq) * per, cols_lo), (per, width))
                term = mm(mix_pieces[k], w)
                acc = term if acc is None else acc + term
            return acc

        if nchan != 4:
            return lax.psum(project(0, out_cols), "chan").astype(BF16)
        core = lax.axis_index("chan") % 2
        width = out_cols // 2
        other = project((1 - core) * width, width)
        got_other = swap(other.astype(BF16), 1)
        mine = project(core * width, width)
        chip = mine + got_other.astype(F32)
        total = (chip + swap(chip.astype(BF16), 2).astype(F32)).astype(BF16)
        peer = swap(total, 1)
        return jnp.where(core == 0, jnp.concatenate([total, peer], 1), jnp.concatenate([peer, total], 1))

    return local


def solution(mesh):
    in_specs = (
        P(("groups", "seq"), "chan"),
        P(("groups", "seq"), "chan"),
        P(("groups", "seq"), "chan"),
        P("chan", None),
        P("chan", None),
        P("chan", None),
        P(("groups", "seq")),
    )
    out_specs = P(("groups", "seq"), None)
    local = make_local(mesh.shape["seq"], mesh.shape["chan"])
    return jax.shard_map(local, mesh=mesh, in_specs=in_specs, out_specs=out_specs, check_vma=False)
```

```python
import functools
import numpy as np
import jax
import jax.numpy as jnp
from jax import lax
from jax.sharding import PartitionSpec as P
from jax.experimental import pallas as pl
from jax.experimental.pallas import tpu as pltpu

F32 = jnp.float32
BF16 = jnp.bfloat16


def split_bf16(mat):
    hi = mat.astype(jnp.bfloat16)
    lo = (mat - hi.astype(np.float64)).astype(jnp.bfloat16)
    return hi, lo


def dft_mats(length):
    half = length // 2
    n = np.arange(length)
    f = np.arange(half)
    ang = 2.0 * np.pi * ((f[:, None] * n[None, :]) % length) / length
    fwd = np.zeros((length, length))
    fwd[:half] = np.cos(ang)
    fwd[half] = np.where(n % 2 == 0, 1.0, -1.0)
    fwd[half + 1:] = -np.sin(ang[1:])
    inv = np.zeros((length, length))
    scale = np.full(half, 2.0)
    scale[0] = 1.0
    inv[:, :half] = (np.cos(ang) * scale[:, None]).T / length
    inv[:, half] = np.where(n % 2 == 0, 1.0, -1.0) / length
    inv[:, half + 1:] = (-2.0 * np.sin(ang[1:])).T / length
    return split_bf16(fwd), split_bf16(inv)


def round_bf16(x, in_kernel):
    if in_kernel:
        return x.astype(BF16).astype(F32)
    return lax.reduce_precision(x, exponent_bits=8, mantissa_bits=7)


def hyena_math(pieces, m0, m1, spec1, spec2, mats, rows, wait, in_kernel):
    nseq = len(pieces)
    per = pieces[0].shape[1]
    length = m0.shape[0]
    half = length // 2
    order = [(nseq - j) % nseq for j in range(nseq)]
    first = jnp.concatenate([pieces[k][0:rows, :] for k in order], axis=0).astype(F32)
    gate = jnp.concatenate([pieces[k][rows:2 * rows, :] for k in order], axis=0).astype(F32)

    def conv(z, spec, first_call):
        masked = jnp.concatenate([z * m0, z * m1], axis=1).astype(BF16)
        if first_call:
            wait(0)
            wait(1)
        x = (jnp.dot(mats[0](), masked, preferred_element_type=F32)
             + jnp.dot(mats[1](), masked, preferred_element_type=F32))
        a, b, d = (jnp.concatenate([v, v], axis=1) for v in (f() for f in spec))
        xr = x[:half]
        xi = x[half:]
        y = jnp.concatenate([xr * a - xi * b, xr * b + xi * d], axis=0)
        y_hi32 = round_bf16(y, in_kernel)
        y_hi = y_hi32.astype(BF16)
        y_lo = (y - y_hi32).astype(BF16)
        if first_call:
            wait(2)
            wait(3)
        ihi = mats[2]()
        both = (jnp.dot(ihi, y_hi, preferred_element_type=F32)
                + jnp.dot(ihi, y_lo, preferred_element_type=F32)
                + jnp.dot(mats[3](), y_hi, preferred_element_type=F32))
        return both[:, :per] * m0 + both[:, per:] * m1

    first_mix = conv(first, spec1, True)
    second_input = round_bf16(gate * first_mix, in_kernel)
    return conv(second_input, spec2, False).astype(BF16)


def hyena_kernel(*refs, nseq, rows):
    pieces = [r[...] for r in refs[:nseq]]
    m0_ref, m1_ref = refs[nseq:nseq + 2]
    spec_refs = refs[nseq + 2:nseq + 8]
    mats_hbm = refs[nseq + 8:nseq + 12]
    o_ref = refs[nseq + 12]
    mats = refs[nseq + 13:nseq + 17]
    sem = refs[nseq + 17]
    copies = [pltpu.make_async_copy(mats_hbm[i], mats[i], sem.at[i]) for i in range(4)]
    for c in copies:
        c.start()
    loader = lambda r: (lambda: r[...])
    spec1 = [loader(r) for r in spec_refs[:3]]
    spec2 = [loader(r) for r in spec_refs[3:]]
    o_ref[...] = hyena_math(pieces, m0_ref[...], m1_ref[...], spec1, spec2,
                            [loader(r) for r in mats], rows, lambda i: copies[i].wait(), True)


def hyena_call(pieces, m0, m1, spec1, spec2, mats, rows):
    nseq = len(pieces)
    length = m0.shape[0]
    per = pieces[0].shape[1]
    if 4 * length * length * 2 > 8 * 1024 * 1024:
        const = lambda v: (lambda: v)
        return hyena_math(pieces, m0, m1, [const(v) for v in spec1], [const(v) for v in spec2],
                          [const(v) for v in mats], rows, lambda i: None, False)
    vmem = pl.BlockSpec(memory_space=pltpu.VMEM)
    hbm = pl.BlockSpec(memory_space=pl.ANY)
    flops = 2 * (2 * length * length * 2 * per * 5)
    return pl.pallas_call(
        functools.partial(hyena_kernel, nseq=nseq, rows=rows),
        out_shape=jax.ShapeDtypeStruct((length, per), BF16),
        in_specs=[vmem] * (nseq + 8) + [hbm] * 4,
        out_specs=vmem,
        scratch_shapes=[pltpu.VMEM((length, length), BF16) for _ in range(4)]
        + [pltpu.SemaphoreType.DMA((4,))],
        compiler_params=pltpu.CompilerParams(vmem_limit_bytes=24 * 1024 * 1024),
        cost_estimate=pl.CostEstimate(flops=flops, transcendentals=0,
                                      bytes_accessed=4 * length * length * 2 + 8 * length * per),
    )(*pieces, m0, m1, *spec1, *spec2, *mats)

def proj_kernel(*refs, nseq):
    src_ref = refs[0]
    pieces = refs[1:1 + nseq]
    w_hbm = refs[1 + nseq]
    o_ref = refs[2 + nseq]
    bufs = refs[3 + nseq:3 + 2 * nseq]
    sem = refs[3 + 2 * nseq]
    per = bufs[0].shape[0]
    copies = [pltpu.make_async_copy(w_hbm.at[pl.ds(src_ref[k] * per, per), :], bufs[k], sem.at[k])
              for k in range(nseq)]
    for c in copies:
        c.start()
    acc = None
    for k in range(nseq):
        copies[k].wait()
        term = jnp.dot(pieces[k][...], bufs[k][...], preferred_element_type=F32)
        acc = term if acc is None else acc + term
    o_ref[...] = acc


def proj_call(srcs, pieces, out_weight):
    nseq = len(pieces)
    rows, per = pieces[0].shape
    out_cols = out_weight.shape[1]
    vmem = pl.BlockSpec(memory_space=pltpu.VMEM)
    return pl.pallas_call(
        functools.partial(proj_kernel, nseq=nseq),
        out_shape=jax.ShapeDtypeStruct((rows, out_cols), F32),
        in_specs=[pl.BlockSpec(memory_space=pltpu.SMEM)] + [vmem] * nseq + [pl.BlockSpec(memory_space=pl.ANY)],
        out_specs=vmem,
        scratch_shapes=[pltpu.VMEM((per, out_cols), BF16) for _ in range(nseq)]
        + [pltpu.SemaphoreType.DMA((nseq,))],
        compiler_params=pltpu.CompilerParams(vmem_limit_bytes=32 * 1024 * 1024),
        cost_estimate=pl.CostEstimate(flops=2 * rows * per * nseq * out_cols, transcendentals=0,
                                      bytes_accessed=per * nseq * out_cols * 2 + rows * out_cols * 4),
    )(srcs, *pieces, out_weight)


def mm(a, b):
    return jnp.dot(a, b, preferred_element_type=F32)


def swap(x, bit):
    return lax.ppermute(x, "chan", [(c, c ^ bit) for c in range(4)])


def make_local(nseq, nchan):
    def local(value, first_gate, second_gate, first_filter, second_filter, out_weight, segment_ids):
        chans = value.shape[1]
        filt_local, length = first_filter.shape
        group = chans // filt_local
        per = chans // nseq
        fpd = per // group
        half = length // 2
        (f_hi, f_lo), (i_hi, i_lo) = dft_mats(length)
        f_hi, f_lo, i_hi, i_lo = (jnp.asarray(m) for m in (f_hi, f_lo, i_hi, i_lo))

        def spectrum(filt):
            mine = lax.dynamic_slice_in_dim(filt, me * fpd, fpd, 0)
            taps = jnp.repeat(mine.T, group, axis=1)
            spec = mm(f_hi, taps) + mm(f_lo, taps)
            re, im = spec[:half], spec[half:]
            row0 = lax.broadcasted_iota(jnp.int32, re.shape, 0) == 0
            a = re
            b = jnp.where(row0, 0.0, im)
            d = jnp.where(row0, im, re)
            return a, b, d

        rows = value.shape[0]
        me = lax.axis_index("seq")
        order = [0] + [k for k in (1, nseq - 1) if k < nseq] + [k for k in range(2, nseq - 1)]
        order = list(dict.fromkeys(order))

        first_input = (first_gate.astype(F32) * value.astype(F32)).astype(BF16)
        id_rows = -(-rows // per)
        pad_rows = -(-id_rows // 16) * 16
        ids = jnp.pad(segment_ids.astype(BF16), (0, pad_rows * per - rows)).reshape(pad_rows, per)

        def block_for(dest):
            cols = lambda x: lax.dynamic_slice_in_dim(x, dest * per, per, 1)
            return jnp.concatenate([cols(first_input), cols(second_gate), ids], axis=0)

        got = {0: block_for(me)}
        for k in order[1:]:
            got[k] = lax.ppermute(block_for((me + k) % nseq), "seq", [(i, (i + k) % nseq) for i in range(nseq)])
        seg_blocks = jnp.stack([got[(nseq - j) % nseq][2 * rows:] for j in range(nseq)])
        segs = seg_blocks.reshape(nseq, pad_rows * per)[:, :rows].reshape(nseq * rows)
        in0 = (segs == 0).astype(F32)[:, None]
        in1 = (segs == 1).astype(F32)[:, None]
        second_mix = hyena_call([got[k] for k in range(nseq)], in0, in1, spectrum(first_filter),
                                spectrum(second_filter), (f_hi, f_lo, i_hi, i_lo), rows)
        mix_pieces = {0: second_mix[:rows]}
        for k in order[1:]:
            mix_pieces[k] = lax.ppermute(second_mix[k * rows:(k + 1) * rows], "seq",
                                         [(i, (i + k) % nseq) for i in range(nseq)])
        out_cols = out_weight.shape[1]

        srcs = jnp.stack([((me - k) % nseq).astype(jnp.int32) for k in range(nseq)])
        partial_out = proj_call(srcs, [mix_pieces[k] for k in range(nseq)], out_weight)

        if nchan != 4:
            return lax.psum(partial_out, "chan").astype(BF16)
        core = lax.axis_index("chan") % 2
        width = out_cols // 2
        other = lax.dynamic_slice_in_dim(partial_out, (1 - core) * width, width, 1)
        got_other = swap(other.astype(BF16), 1)
        mine = lax.dynamic_slice_in_dim(partial_out, core * width, width, 1)
        chip = mine + got_other.astype(F32)
        total = (chip + swap(chip.astype(BF16), 2).astype(F32)).astype(BF16)
        peer = swap(total, 1)
        return jnp.where(core == 0, jnp.concatenate([total, peer], 1), jnp.concatenate([peer, total], 1))

    return local


def solution(mesh):
    in_specs = (
        P(("groups", "seq"), "chan"),
        P(("groups", "seq"), "chan"),
        P(("groups", "seq"), "chan"),
        P("chan", None),
        P("chan", None),
        P("chan", None),
        P(("groups", "seq")),
    )
    out_specs = P(("groups", "seq"), None)
    local = make_local(mesh.shape["seq"], mesh.shape["chan"])
    return jax.shard_map(local, mesh=mesh, in_specs=in_specs, out_specs=out_specs, check_vma=False)
```

```python
import functools
import numpy as np
import jax
import jax.numpy as jnp
from jax import lax
from jax.sharding import PartitionSpec as P
from jax.experimental import pallas as pl
from jax.experimental.pallas import tpu as pltpu

F32 = jnp.float32
BF16 = jnp.bfloat16


def split_bf16(mat):
    hi = mat.astype(jnp.bfloat16)
    lo = (mat - hi.astype(np.float64)).astype(jnp.bfloat16)
    return hi, lo


def dft_mats(length):
    half = length // 2
    n = np.arange(length)
    f = np.arange(half)
    ang = 2.0 * np.pi * ((f[:, None] * n[None, :]) % length) / length
    fwd = np.zeros((length, length))
    fwd[:half] = np.cos(ang)
    fwd[half] = np.where(n % 2 == 0, 1.0, -1.0)
    fwd[half + 1:] = -np.sin(ang[1:])
    inv = np.zeros((length, length))
    scale = np.full(half, 2.0)
    scale[0] = 1.0
    inv[:, :half] = (np.cos(ang) * scale[:, None]).T / length
    inv[:, half] = np.where(n % 2 == 0, 1.0, -1.0) / length
    inv[:, half + 1:] = (-2.0 * np.sin(ang[1:])).T / length
    return split_bf16(fwd), split_bf16(inv)


def round_bf16(x, in_kernel):
    if in_kernel:
        return x.astype(BF16).astype(F32)
    return lax.reduce_precision(x, exponent_bits=8, mantissa_bits=7)


def hyena_math(pieces, m0, m1, spec1, spec2, mats, rows, wait, in_kernel):
    nseq = len(pieces)
    per = pieces[0].shape[1]
    length = m0.shape[0]
    half = length // 2
    order = [(nseq - j) % nseq for j in range(nseq)]
    first = jnp.concatenate([pieces[k][0:rows, :] for k in order], axis=0).astype(F32)
    gate = jnp.concatenate([pieces[k][rows:2 * rows, :] for k in order], axis=0).astype(F32)

    def conv(z, spec, first_call):
        masked = jnp.concatenate([z * m0, z * m1], axis=1).astype(BF16)
        if first_call:
            wait(0)
            wait(1)
        x = (jnp.dot(mats[0](), masked, preferred_element_type=F32)
             + jnp.dot(mats[1](), masked, preferred_element_type=F32))
        a, b, d = (jnp.concatenate([v, v], axis=1) for v in (f() for f in spec))
        xr = x[:half]
        xi = x[half:]
        y = jnp.concatenate([xr * a - xi * b, xr * b + xi * d], axis=0)
        y_hi32 = round_bf16(y, in_kernel)
        y_hi = y_hi32.astype(BF16)
        y_lo = (y - y_hi32).astype(BF16)
        if first_call:
            wait(2)
            wait(3)
        ihi = mats[2]()
        both = (jnp.dot(ihi, y_hi, preferred_element_type=F32)
                + jnp.dot(ihi, y_lo, preferred_element_type=F32)
                + jnp.dot(mats[3](), y_hi, preferred_element_type=F32))
        return both[:, :per] * m0 + both[:, per:] * m1

    first_mix = conv(first, spec1, True)
    second_input = round_bf16(gate * first_mix, in_kernel)
    return conv(second_input, spec2, False).astype(BF16)


def hyena_kernel(*refs, nseq, rows):
    pieces = [r[...] for r in refs[:nseq]]
    m0_ref, m1_ref = refs[nseq:nseq + 2]
    spec_refs = refs[nseq + 2:nseq + 8]
    mats_hbm = refs[nseq + 8:nseq + 12]
    w_hbm = refs[nseq + 12]
    o_ref, w_out = refs[nseq + 13:nseq + 15]
    mats = refs[nseq + 15:nseq + 19]
    sem = refs[nseq + 19]
    copies = [pltpu.make_async_copy(mats_hbm[i], mats[i], sem.at[i]) for i in range(4)]
    w_copy = pltpu.make_async_copy(w_hbm, w_out, sem.at[4])
    for c in copies:
        c.start()
    w_copy.start()
    loader = lambda r: (lambda: r[...])
    spec1 = [loader(r) for r in spec_refs[:3]]
    spec2 = [loader(r) for r in spec_refs[3:]]
    o_ref[...] = hyena_math(pieces, m0_ref[...], m1_ref[...], spec1, spec2,
                            [loader(r) for r in mats], rows, lambda i: copies[i].wait(), True)
    w_copy.wait()


def hyena_call(pieces, m0, m1, spec1, spec2, mats, rows, out_weight):
    nseq = len(pieces)
    length = m0.shape[0]
    per = pieces[0].shape[1]
    if 4 * length * length * 2 > 8 * 1024 * 1024:
        const = lambda v: (lambda: v)
        return hyena_math(pieces, m0, m1, [const(v) for v in spec1], [const(v) for v in spec2],
                          [const(v) for v in mats], rows, lambda i: None, False), out_weight
    vmem = pl.BlockSpec(memory_space=pltpu.VMEM)
    hbm = pl.BlockSpec(memory_space=pltpu.MemorySpace.HBM)
    flops = 2 * (2 * length * length * 2 * per * 5)
    return pl.pallas_call(
        functools.partial(hyena_kernel, nseq=nseq, rows=rows),
        out_shape=(jax.ShapeDtypeStruct((length, per), BF16),
                   jax.ShapeDtypeStruct(out_weight.shape, out_weight.dtype)),
        in_specs=[vmem] * (nseq + 8) + [hbm] * 5,
        out_specs=(vmem, vmem),
        scratch_shapes=[pltpu.VMEM((length, length), BF16) for _ in range(4)]
        + [pltpu.SemaphoreType.DMA((5,))],
        compiler_params=pltpu.CompilerParams(vmem_limit_bytes=40 * 1024 * 1024),
        cost_estimate=pl.CostEstimate(flops=flops, transcendentals=0,
                                      bytes_accessed=4 * length * length * 2 + 8 * length * per),
    )(*pieces, m0, m1, *spec1, *spec2, *mats, out_weight)

def proj_kernel(*refs, nseq):
    src_ref = refs[0]
    pieces = refs[1:1 + nseq]
    w_ref = refs[1 + nseq]
    o_ref = refs[2 + nseq]
    per = pieces[0].shape[1]
    acc = None
    for k in range(nseq):
        start = pl.multiple_of(src_ref[k] * per, per)
        term = jnp.dot(pieces[k][...], w_ref[pl.ds(start, per), :], preferred_element_type=F32)
        acc = term if acc is None else acc + term
    o_ref[...] = acc


def proj_call(srcs, pieces, out_weight):
    nseq = len(pieces)
    rows, per = pieces[0].shape
    out_cols = out_weight.shape[1]
    vmem = pl.BlockSpec(memory_space=pltpu.VMEM)
    return pl.pallas_call(
        functools.partial(proj_kernel, nseq=nseq),
        out_shape=jax.ShapeDtypeStruct((rows, out_cols), F32),
        in_specs=[pl.BlockSpec(memory_space=pltpu.SMEM)] + [vmem] * (nseq + 1),
        out_specs=vmem,
        compiler_params=pltpu.CompilerParams(vmem_limit_bytes=24 * 1024 * 1024),
        cost_estimate=pl.CostEstimate(flops=2 * rows * per * nseq * out_cols, transcendentals=0,
                                      bytes_accessed=per * nseq * out_cols * 2 + rows * out_cols * 4),
    )(srcs, *pieces, out_weight)


def mm(a, b):
    return jnp.dot(a, b, preferred_element_type=F32)


def swap(x, bit):
    return lax.ppermute(x, "chan", [(c, c ^ bit) for c in range(4)])


def make_local(nseq, nchan):
    def local(value, first_gate, second_gate, first_filter, second_filter, out_weight, segment_ids):
        chans = value.shape[1]
        filt_local, length = first_filter.shape
        group = chans // filt_local
        per = chans // nseq
        fpd = per // group
        half = length // 2
        (f_hi, f_lo), (i_hi, i_lo) = dft_mats(length)
        f_hi, f_lo, i_hi, i_lo = (jnp.asarray(m) for m in (f_hi, f_lo, i_hi, i_lo))

        def spectrum(filt):
            mine = lax.dynamic_slice_in_dim(filt, me * fpd, fpd, 0)
            taps = jnp.repeat(mine.T, group, axis=1)
            spec = mm(f_hi, taps) + mm(f_lo, taps)
            re, im = spec[:half], spec[half:]
            row0 = lax.broadcasted_iota(jnp.int32, re.shape, 0) == 0
            a = re
            b = jnp.where(row0, 0.0, im)
            d = jnp.where(row0, im, re)
            return a, b, d

        rows = value.shape[0]
        me = lax.axis_index("seq")
        order = [0] + [k for k in (1, nseq - 1) if k < nseq] + [k for k in range(2, nseq - 1)]
        order = list(dict.fromkeys(order))

        first_input = (first_gate.astype(F32) * value.astype(F32)).astype(BF16)
        id_rows = -(-rows // per)
        pad_rows = -(-id_rows // 16) * 16
        ids = jnp.pad(segment_ids.astype(BF16), (0, pad_rows * per - rows)).reshape(pad_rows, per)

        def block_for(dest):
            cols = lambda x: lax.dynamic_slice_in_dim(x, dest * per, per, 1)
            return jnp.concatenate([cols(first_input), cols(second_gate), ids], axis=0)

        got = {0: block_for(me)}
        for k in order[1:]:
            got[k] = lax.ppermute(block_for((me + k) % nseq), "seq", [(i, (i + k) % nseq) for i in range(nseq)])
        seg_blocks = jnp.stack([got[(nseq - j) % nseq][2 * rows:] for j in range(nseq)])
        segs = seg_blocks.reshape(nseq, pad_rows * per)[:, :rows].reshape(nseq * rows)
        in0 = (segs == 0).astype(F32)[:, None]
        in1 = (segs == 1).astype(F32)[:, None]
        second_mix, staged_weight = hyena_call(
            [got[k] for k in range(nseq)], in0, in1, spectrum(first_filter),
            spectrum(second_filter), (f_hi, f_lo, i_hi, i_lo), rows, out_weight)
        mix_pieces = {0: second_mix[:rows]}
        for k in order[1:]:
            mix_pieces[k] = lax.ppermute(second_mix[k * rows:(k + 1) * rows], "seq",
                                         [(i, (i + k) % nseq) for i in range(nseq)])
        out_cols = out_weight.shape[1]

        srcs = jnp.stack([((me - k) % nseq).astype(jnp.int32) for k in range(nseq)])
        partial_out = proj_call(srcs, [mix_pieces[k] for k in range(nseq)], staged_weight)

        if nchan != 4:
            return lax.psum(partial_out, "chan").astype(BF16)
        core = lax.axis_index("chan") % 2
        width = out_cols // 2
        other = lax.dynamic_slice_in_dim(partial_out, (1 - core) * width, width, 1)
        got_other = swap(other.astype(BF16), 1)
        mine = lax.dynamic_slice_in_dim(partial_out, core * width, width, 1)
        chip = mine + got_other.astype(F32)
        total = (chip + swap(chip.astype(BF16), 2).astype(F32)).astype(BF16)
        peer = swap(total, 1)
        return jnp.where(core == 0, jnp.concatenate([total, peer], 1), jnp.concatenate([peer, total], 1))

    return local


def solution(mesh):
    in_specs = (
        P(("groups", "seq"), "chan"),
        P(("groups", "seq"), "chan"),
        P(("groups", "seq"), "chan"),
        P("chan", None),
        P("chan", None),
        P("chan", None),
        P(("groups", "seq")),
    )
    out_specs = P(("groups", "seq"), None)
    local = make_local(mesh.shape["seq"], mesh.shape["chan"])
    return jax.shard_map(local, mesh=mesh, in_specs=in_specs, out_specs=out_specs, check_vma=False)
```

```python
import functools
import numpy as np
import jax
import jax.numpy as jnp
from jax import lax
from jax.sharding import PartitionSpec as P
from jax.experimental import pallas as pl
from jax.experimental.pallas import tpu as pltpu

F32 = jnp.float32
BF16 = jnp.bfloat16


def split_bf16(mat):
    hi = mat.astype(jnp.bfloat16)
    lo = (mat - hi.astype(np.float64)).astype(jnp.bfloat16)
    return hi, lo


def dft_mats(length):
    half = length // 2
    n = np.arange(length)
    f = np.arange(half)
    ang = 2.0 * np.pi * ((f[:, None] * n[None, :]) % length) / length
    fwd = np.zeros((length, length))
    fwd[:half] = np.cos(ang)
    fwd[half] = np.where(n % 2 == 0, 1.0, -1.0)
    fwd[half + 1:] = -np.sin(ang[1:])
    inv = np.zeros((length, length))
    scale = np.full(half, 2.0)
    scale[0] = 1.0
    inv[:, :half] = (np.cos(ang) * scale[:, None]).T / length
    inv[:, half] = np.where(n % 2 == 0, 1.0, -1.0) / length
    inv[:, half + 1:] = (-2.0 * np.sin(ang[1:])).T / length
    return split_bf16(fwd), split_bf16(inv)


def round_bf16(x, in_kernel):
    if in_kernel:
        return x.astype(BF16).astype(F32)
    return lax.reduce_precision(x, exponent_bits=8, mantissa_bits=7)


def hyena_math(pieces, m0, m1, spec1, spec2, mats, rows, wait, in_kernel):
    nseq = len(pieces)
    per = pieces[0].shape[1]
    length = m0.shape[0]
    half = length // 2
    order = [(nseq - j) % nseq for j in range(nseq)]
    first = jnp.concatenate([pieces[k][0:rows, :] for k in order], axis=0).astype(F32)
    gate = jnp.concatenate([pieces[k][rows:2 * rows, :] for k in order], axis=0).astype(F32)

    def conv(z, spec, first_call):
        masked = jnp.concatenate([z * m0, z * m1], axis=1).astype(BF16)
        if first_call:
            wait(0)
            wait(1)
        x = (jnp.dot(mats[0](), masked, preferred_element_type=F32)
             + jnp.dot(mats[1](), masked, preferred_element_type=F32))
        a, b, d = (jnp.concatenate([v, v], axis=1) for v in (f() for f in spec))
        xr = x[:half]
        xi = x[half:]
        y = jnp.concatenate([xr * a - xi * b, xr * b + xi * d], axis=0)
        y_hi32 = round_bf16(y, in_kernel)
        y_hi = y_hi32.astype(BF16)
        y_lo = (y - y_hi32).astype(BF16)
        if first_call:
            wait(2)
            wait(3)
        ihi = mats[2]()
        both = (jnp.dot(ihi, y_hi, preferred_element_type=F32)
                + jnp.dot(ihi, y_lo, preferred_element_type=F32)
                + jnp.dot(mats[3](), y_hi, preferred_element_type=F32))
        return both[:, :per] * m0 + both[:, per:] * m1

    first_mix = conv(first, spec1, True)
    second_input = round_bf16(gate * first_mix, in_kernel)
    return conv(second_input, spec2, False).astype(BF16)


def hyena_kernel(*refs, nseq, rows):
    pieces = [r[...] for r in refs[:nseq]]
    m0_ref, m1_ref = refs[nseq:nseq + 2]
    spec_refs = refs[nseq + 2:nseq + 8]
    mats_hbm = refs[nseq + 8:nseq + 12]
    w_hbm = refs[nseq + 12]
    o_ref, w_out = refs[nseq + 13:nseq + 15]
    mats = refs[nseq + 15:nseq + 19]
    sem = refs[nseq + 19]
    copies = [pltpu.make_async_copy(mats_hbm[i], mats[i], sem.at[i]) for i in range(4)]
    w_copy = pltpu.make_async_copy(w_hbm, w_out, sem.at[4])
    for c in copies:
        c.start()
    w_copy.start()
    loader = lambda r: (lambda: r[...])
    spec1 = [loader(r) for r in spec_refs[:3]]
    spec2 = [loader(r) for r in spec_refs[3:]]
    o_ref[...] = hyena_math(pieces, m0_ref[...], m1_ref[...], spec1, spec2,
                            [loader(r) for r in mats], rows, lambda i: copies[i].wait(), True)
    w_copy.wait()


def hyena_call(pieces, m0, m1, spec1, spec2, mats, rows, out_weight):
    nseq = len(pieces)
    length = m0.shape[0]
    per = pieces[0].shape[1]
    if 4 * length * length * 2 > 8 * 1024 * 1024:
        const = lambda v: (lambda: v)
        return hyena_math(pieces, m0, m1, [const(v) for v in spec1], [const(v) for v in spec2],
                          [const(v) for v in mats], rows, lambda i: None, False), out_weight
    vmem = pl.BlockSpec(memory_space=pltpu.VMEM)
    hbm = pl.BlockSpec(memory_space=pltpu.MemorySpace.HBM)
    flops = 2 * (2 * length * length * 2 * per * 5)
    return pl.pallas_call(
        functools.partial(hyena_kernel, nseq=nseq, rows=rows),
        out_shape=(jax.ShapeDtypeStruct((length, per), BF16),
                   jax.ShapeDtypeStruct(out_weight.shape, out_weight.dtype)),
        in_specs=[vmem] * (nseq + 8) + [hbm] * 5,
        out_specs=(vmem, vmem),
        scratch_shapes=[pltpu.VMEM((length, length), BF16) for _ in range(4)]
        + [pltpu.SemaphoreType.DMA((5,))],
        compiler_params=pltpu.CompilerParams(vmem_limit_bytes=40 * 1024 * 1024),
        cost_estimate=pl.CostEstimate(flops=flops, transcendentals=0,
                                      bytes_accessed=4 * length * length * 2 + 8 * length * per),
    )(*pieces, m0, m1, *spec1, *spec2, *mats, out_weight)

def proj_kernel(*refs, nseq):
    src_ref = refs[0]
    pieces = refs[1:1 + nseq]
    w_ref = refs[1 + nseq]
    o_ref = refs[2 + nseq]
    per = pieces[0].shape[1]
    acc = None
    for k in range(nseq):
        start = pl.multiple_of(src_ref[k] * per, per)
        term = jnp.dot(pieces[k][...], w_ref[pl.ds(start, per), :], preferred_element_type=F32)
        acc = term if acc is None else acc + term
    o_ref[...] = acc


def proj_call(srcs, pieces, out_weight):
    nseq = len(pieces)
    rows, per = pieces[0].shape
    out_cols = out_weight.shape[1]
    vmem = pl.BlockSpec(memory_space=pltpu.VMEM)
    return pl.pallas_call(
        functools.partial(proj_kernel, nseq=nseq),
        out_shape=jax.ShapeDtypeStruct((rows, out_cols), F32),
        in_specs=[pl.BlockSpec(memory_space=pltpu.SMEM)] + [vmem] * (nseq + 1),
        out_specs=vmem,
        compiler_params=pltpu.CompilerParams(vmem_limit_bytes=24 * 1024 * 1024),
        cost_estimate=pl.CostEstimate(flops=2 * rows * per * nseq * out_cols, transcendentals=0,
                                      bytes_accessed=per * nseq * out_cols * 2 + rows * out_cols * 4),
    )(srcs, *pieces, out_weight)


def mm(a, b):
    return jnp.dot(a, b, preferred_element_type=F32)


def swap(x, bit):
    return lax.ppermute(x, "chan", [(c, c ^ bit) for c in range(4)])


def make_local(nseq, nchan):
    def local(value, first_gate, second_gate, first_filter, second_filter, out_weight, segment_ids):
        chans = value.shape[1]
        filt_local, length = first_filter.shape
        group = chans // filt_local
        per = chans // nseq
        fpd = per // group
        half = length // 2
        (f_hi, f_lo), (i_hi, i_lo) = dft_mats(length)
        f_hi, f_lo, i_hi, i_lo = (jnp.asarray(m) for m in (f_hi, f_lo, i_hi, i_lo))

        def spectrum(filt):
            mine = lax.dynamic_slice_in_dim(filt, me * fpd, fpd, 0)
            taps = jnp.repeat(mine.T, group, axis=1)
            spec = mm(f_hi, taps) + mm(f_lo, taps)
            re, im = spec[:half], spec[half:]
            row0 = lax.broadcasted_iota(jnp.int32, re.shape, 0) == 0
            a = re
            b = jnp.where(row0, 0.0, im)
            d = jnp.where(row0, im, re)
            return a, b, d

        rows = value.shape[0]
        me = lax.axis_index("seq")
        order = [0] + [k for k in (1, nseq - 1) if k < nseq] + [k for k in range(2, nseq - 1)]
        order = list(dict.fromkeys(order))

        first_input = (first_gate.astype(F32) * value.astype(F32)).astype(BF16)
        id_rows = -(-rows // per)
        pad_rows = -(-id_rows // 16) * 16
        ids = jnp.pad(segment_ids.astype(BF16), (0, pad_rows * per - rows)).reshape(pad_rows, per)

        def block_for(dest):
            cols = lambda x: lax.dynamic_slice_in_dim(x, dest * per, per, 1)
            return jnp.concatenate([cols(first_input), cols(second_gate), ids], axis=0)

        got = {0: block_for(me)}
        for k in order[1:]:
            got[k] = lax.ppermute(block_for((me + k) % nseq), "seq", [(i, (i + k) % nseq) for i in range(nseq)])
        seg_blocks = jnp.stack([got[(nseq - j) % nseq][2 * rows:] for j in range(nseq)])
        segs = seg_blocks.reshape(nseq, pad_rows * per)[:, :rows].reshape(nseq * rows)
        in0 = (segs == 0).astype(F32)[:, None]
        in1 = (segs == 1).astype(F32)[:, None]
        second_mix, staged_weight = hyena_call(
            [got[k] for k in range(nseq)], in0, in1, spectrum(first_filter),
            spectrum(second_filter), (f_hi, f_lo, i_hi, i_lo), rows, out_weight)
        out_cols = out_weight.shape[1]
        srcs = jnp.stack([((me - k) % nseq).astype(jnp.int32) for k in range(nseq)])
        core = lax.axis_index("chan") % 2
        width = out_cols // 2
        chunks = 2 if (nchan == 4 and rows % 32 == 0) else 1
        step = rows // chunks
        results = []
        for c in range(chunks):
            lo = c * step
            pieces = {0: second_mix[lo:lo + step]}
            for k in order[1:]:
                base = k * rows + lo
                pieces[k] = lax.ppermute(second_mix[base:base + step], "seq",
                                         [(i, (i + k) % nseq) for i in range(nseq)])
            partial_out = proj_call(srcs, [pieces[k] for k in range(nseq)], staged_weight)
            if nchan != 4:
                results.append(lax.psum(partial_out, "chan").astype(BF16))
                continue
            other = lax.dynamic_slice_in_dim(partial_out, (1 - core) * width, width, 1)
            got_other = swap(other.astype(BF16), 1)
            mine = lax.dynamic_slice_in_dim(partial_out, core * width, width, 1)
            chip = mine + got_other.astype(F32)
            total = (chip + swap(chip.astype(BF16), 2).astype(F32)).astype(BF16)
            peer = swap(total, 1)
            results.append(jnp.where(core == 0, jnp.concatenate([total, peer], 1),
                                     jnp.concatenate([peer, total], 1)))
        return jnp.concatenate(results, axis=0)

    return local


def solution(mesh):
    in_specs = (
        P(("groups", "seq"), "chan"),
        P(("groups", "seq"), "chan"),
        P(("groups", "seq"), "chan"),
        P("chan", None),
        P("chan", None),
        P("chan", None),
        P(("groups", "seq")),
    )
    out_specs = P(("groups", "seq"), None)
    local = make_local(mesh.shape["seq"], mesh.shape["chan"])
    return jax.shard_map(local, mesh=mesh, in_specs=in_specs, out_specs=out_specs, check_vma=False)
```

```python
import functools
import numpy as np
import jax
import jax.numpy as jnp
from jax import lax
from jax.sharding import PartitionSpec as P
from jax.experimental import pallas as pl
from jax.experimental.pallas import tpu as pltpu

F32 = jnp.float32
BF16 = jnp.bfloat16


def split_bf16(mat):
    hi = mat.astype(jnp.bfloat16)
    lo = (mat - hi.astype(np.float64)).astype(jnp.bfloat16)
    return hi, lo


def dft_mats(length):
    half = length // 2
    n = np.arange(length)
    f = np.arange(half)
    ang = 2.0 * np.pi * ((f[:, None] * n[None, :]) % length) / length
    fwd = np.zeros((length, length))
    fwd[:half] = np.cos(ang)
    fwd[half] = np.where(n % 2 == 0, 1.0, -1.0)
    fwd[half + 1:] = -np.sin(ang[1:])
    inv = np.zeros((length, length))
    scale = np.full(half, 2.0)
    scale[0] = 1.0
    inv[:, :half] = (np.cos(ang) * scale[:, None]).T / length
    inv[:, half] = np.where(n % 2 == 0, 1.0, -1.0) / length
    inv[:, half + 1:] = (-2.0 * np.sin(ang[1:])).T / length
    return split_bf16(fwd), split_bf16(inv)


def mm_t(a, b):
    return lax.dot_general(a, b, (((0,), (0,)), ((), ())), preferred_element_type=F32)


def round_bf16(x, in_kernel):
    if in_kernel:
        return x.astype(BF16).astype(F32)
    return lax.reduce_precision(x, exponent_bits=8, mantissa_bits=7)


def hyena_math(pieces, m0, m1, spec1, spec2, mats, rows, wait, in_kernel):
    nseq = len(pieces)
    per = pieces[0].shape[1]
    length = m0.shape[0]
    half = length // 2
    order = [(nseq - j) % nseq for j in range(nseq)]
    first = jnp.concatenate([pieces[k][0:rows, :] for k in order], axis=0).astype(F32)
    gate = jnp.concatenate([pieces[k][rows:2 * rows, :] for k in order], axis=0).astype(F32)

    def conv(z, spec, first_call):
        masked = jnp.concatenate([z * m0, z * m1], axis=1).astype(BF16)
        if first_call:
            wait(0)
            wait(1)
        x = (jnp.dot(mats[0](), masked, preferred_element_type=F32)
             + jnp.dot(mats[1](), masked, preferred_element_type=F32))
        a, b, d = (jnp.concatenate([v, v], axis=1) for v in (f() for f in spec))
        xr = x[:half]
        xi = x[half:]
        row = lax.broadcasted_iota(jnp.int32, (length, 1), 0)
        weight = jnp.where((row == 0) | (row == half), 1.0 / length, 2.0 / length).astype(F32)
        y = jnp.concatenate([xr * a - xi * b, xr * b + xi * d], axis=0) * weight
        y_hi32 = round_bf16(y, in_kernel)
        y_hi = y_hi32.astype(BF16)
        y_lo = (y - y_hi32).astype(BF16)
        fhi = mats[0]()
        both = mm_t(fhi, y_hi) + mm_t(fhi, y_lo) + mm_t(mats[1](), y_hi)
        return both[:, :per] * m0 + both[:, per:] * m1

    first_mix = conv(first, spec1, True)
    second_input = round_bf16(gate * first_mix, in_kernel)
    return conv(second_input, spec2, False).astype(BF16)


def hyena_kernel(*refs, nseq, rows):
    pieces = [r[...] for r in refs[:nseq]]
    m0_ref, m1_ref = refs[nseq:nseq + 2]
    spec_refs = refs[nseq + 2:nseq + 8]
    mats_hbm = refs[nseq + 8:nseq + 10]
    w_hbm = refs[nseq + 10]
    o_ref, w_out = refs[nseq + 11:nseq + 13]
    mats = refs[nseq + 13:nseq + 15]
    sem = refs[nseq + 15]
    copies = [pltpu.make_async_copy(mats_hbm[i], mats[i], sem.at[i]) for i in range(2)]
    w_copy = pltpu.make_async_copy(w_hbm, w_out, sem.at[2])
    for c in copies:
        c.start()
    w_copy.start()
    loader = lambda r: (lambda: r[...])
    spec1 = [loader(r) for r in spec_refs[:3]]
    spec2 = [loader(r) for r in spec_refs[3:]]
    o_ref[...] = hyena_math(pieces, m0_ref[...], m1_ref[...], spec1, spec2,
                            [loader(r) for r in mats], rows, lambda i: copies[i].wait(), True)
    w_copy.wait()


def hyena_call(pieces, m0, m1, spec1, spec2, mats, rows, out_weight):
    nseq = len(pieces)
    length = m0.shape[0]
    per = pieces[0].shape[1]
    if 4 * length * length * 2 > 8 * 1024 * 1024:
        const = lambda v: (lambda: v)
        return hyena_math(pieces, m0, m1, [const(v) for v in spec1], [const(v) for v in spec2],
                          [const(v) for v in mats], rows, lambda i: None, False), out_weight
    vmem = pl.BlockSpec(memory_space=pltpu.VMEM)
    hbm = pl.BlockSpec(memory_space=pltpu.MemorySpace.HBM)
    flops = 2 * (2 * length * length * 2 * per * 5)
    return pl.pallas_call(
        functools.partial(hyena_kernel, nseq=nseq, rows=rows),
        out_shape=(jax.ShapeDtypeStruct((length, per), BF16),
                   jax.ShapeDtypeStruct(out_weight.shape, out_weight.dtype)),
        in_specs=[vmem] * (nseq + 8) + [hbm] * 3,
        out_specs=(vmem, vmem),
        scratch_shapes=[pltpu.VMEM((length, length), BF16) for _ in range(2)]
        + [pltpu.SemaphoreType.DMA((3,))],
        compiler_params=pltpu.CompilerParams(vmem_limit_bytes=40 * 1024 * 1024),
        cost_estimate=pl.CostEstimate(flops=flops, transcendentals=0,
                                      bytes_accessed=4 * length * length * 2 + 8 * length * per),
    )(*pieces, m0, m1, *spec1, *spec2, *mats, out_weight)

def proj_kernel(*refs, nseq):
    src_ref = refs[0]
    pieces = refs[1:1 + nseq]
    w_ref = refs[1 + nseq]
    o_ref = refs[2 + nseq]
    per = pieces[0].shape[1]
    acc = None
    for k in range(nseq):
        start = pl.multiple_of(src_ref[k] * per, per)
        term = jnp.dot(pieces[k][...], w_ref[pl.ds(start, per), :], preferred_element_type=F32)
        acc = term if acc is None else acc + term
    o_ref[...] = acc


def proj_call(srcs, pieces, out_weight):
    nseq = len(pieces)
    rows, per = pieces[0].shape
    out_cols = out_weight.shape[1]
    vmem = pl.BlockSpec(memory_space=pltpu.VMEM)
    return pl.pallas_call(
        functools.partial(proj_kernel, nseq=nseq),
        out_shape=jax.ShapeDtypeStruct((rows, out_cols), F32),
        in_specs=[pl.BlockSpec(memory_space=pltpu.SMEM)] + [vmem] * (nseq + 1),
        out_specs=vmem,
        compiler_params=pltpu.CompilerParams(vmem_limit_bytes=24 * 1024 * 1024),
        cost_estimate=pl.CostEstimate(flops=2 * rows * per * nseq * out_cols, transcendentals=0,
                                      bytes_accessed=per * nseq * out_cols * 2 + rows * out_cols * 4),
    )(srcs, *pieces, out_weight)


def mm(a, b):
    return jnp.dot(a, b, preferred_element_type=F32)


def swap(x, bit):
    return lax.ppermute(x, "chan", [(c, c ^ bit) for c in range(4)])


def make_local(nseq, nchan):
    def local(value, first_gate, second_gate, first_filter, second_filter, out_weight, segment_ids):
        chans = value.shape[1]
        filt_local, length = first_filter.shape
        group = chans // filt_local
        per = chans // nseq
        fpd = per // group
        half = length // 2
        (f_hi, f_lo), (i_hi, i_lo) = dft_mats(length)
        f_hi, f_lo, i_hi, i_lo = (jnp.asarray(m) for m in (f_hi, f_lo, i_hi, i_lo))

        def spectrum(filt):
            mine = lax.dynamic_slice_in_dim(filt, me * fpd, fpd, 0)
            taps = jnp.repeat(mine.T, group, axis=1)
            spec = mm(f_hi, taps) + mm(f_lo, taps)
            re, im = spec[:half], spec[half:]
            row0 = lax.broadcasted_iota(jnp.int32, re.shape, 0) == 0
            a = re
            b = jnp.where(row0, 0.0, im)
            d = jnp.where(row0, im, re)
            return a, b, d

        rows = value.shape[0]
        me = lax.axis_index("seq")
        order = [0] + [k for k in (1, nseq - 1) if k < nseq] + [k for k in range(2, nseq - 1)]
        order = list(dict.fromkeys(order))

        first_input = (first_gate.astype(F32) * value.astype(F32)).astype(BF16)
        id_rows = -(-rows // per)
        pad_rows = -(-id_rows // 16) * 16
        ids = jnp.pad(segment_ids.astype(BF16), (0, pad_rows * per - rows)).reshape(pad_rows, per)

        def block_for(dest):
            cols = lambda x: lax.dynamic_slice_in_dim(x, dest * per, per, 1)
            return jnp.concatenate([cols(first_input), cols(second_gate), ids], axis=0)

        got = {0: block_for(me)}
        for k in order[1:]:
            got[k] = lax.ppermute(block_for((me + k) % nseq), "seq", [(i, (i + k) % nseq) for i in range(nseq)])
        seg_blocks = jnp.stack([got[(nseq - j) % nseq][2 * rows:] for j in range(nseq)])
        segs = seg_blocks.reshape(nseq, pad_rows * per)[:, :rows].reshape(nseq * rows)
        in0 = (segs == 0).astype(F32)[:, None]
        in1 = (segs == 1).astype(F32)[:, None]
        second_mix, staged_weight = hyena_call(
            [got[k] for k in range(nseq)], in0, in1, spectrum(first_filter),
            spectrum(second_filter), (f_hi, f_lo), rows, out_weight)
        mix_pieces = {0: second_mix[:rows]}
        for k in order[1:]:
            mix_pieces[k] = lax.ppermute(second_mix[k * rows:(k + 1) * rows], "seq",
                                         [(i, (i + k) % nseq) for i in range(nseq)])
        out_cols = out_weight.shape[1]

        srcs = jnp.stack([((me - k) % nseq).astype(jnp.int32) for k in range(nseq)])
        partial_out = proj_call(srcs, [mix_pieces[k] for k in range(nseq)], staged_weight)

        if nchan != 4:
            return lax.psum(partial_out, "chan").astype(BF16)
        core = lax.axis_index("chan") % 2
        width = out_cols // 2
        other = lax.dynamic_slice_in_dim(partial_out, (1 - core) * width, width, 1)
        got_other = swap(other.astype(BF16), 1)
        mine = lax.dynamic_slice_in_dim(partial_out, core * width, width, 1)
        chip = mine + got_other.astype(F32)
        total = (chip + swap(chip.astype(BF16), 2).astype(F32)).astype(BF16)
        peer = swap(total, 1)
        return jnp.where(core == 0, jnp.concatenate([total, peer], 1), jnp.concatenate([peer, total], 1))

    return local


def solution(mesh):
    in_specs = (
        P(("groups", "seq"), "chan"),
        P(("groups", "seq"), "chan"),
        P(("groups", "seq"), "chan"),
        P("chan", None),
        P("chan", None),
        P("chan", None),
        P(("groups", "seq")),
    )
    out_specs = P(("groups", "seq"), None)
    local = make_local(mesh.shape["seq"], mesh.shape["chan"])
    return jax.shard_map(local, mesh=mesh, in_specs=in_specs, out_specs=out_specs, check_vma=False)
```

```python
import functools
import numpy as np
import jax
import jax.numpy as jnp
from jax import lax
from jax.sharding import PartitionSpec as P
from jax.experimental import pallas as pl
from jax.experimental.pallas import tpu as pltpu

F32 = jnp.float32
BF16 = jnp.bfloat16


def split_bf16(mat):
    hi = mat.astype(jnp.bfloat16)
    lo = (mat - hi.astype(np.float64)).astype(jnp.bfloat16)
    return hi, lo


def dft_mats(length):
    half = length // 2
    n = np.arange(length)
    f = np.arange(half)
    ang = 2.0 * np.pi * ((f[:, None] * n[None, :]) % length) / length
    fwd = np.zeros((length, length))
    fwd[:half] = np.cos(ang)
    fwd[half] = np.where(n % 2 == 0, 1.0, -1.0)
    fwd[half + 1:] = -np.sin(ang[1:])
    inv = np.zeros((length, length))
    scale = np.full(half, 2.0)
    scale[0] = 1.0
    inv[:, :half] = (np.cos(ang) * scale[:, None]).T / length
    inv[:, half] = np.where(n % 2 == 0, 1.0, -1.0) / length
    inv[:, half + 1:] = (-2.0 * np.sin(ang[1:])).T / length
    return split_bf16(fwd), split_bf16(inv)


def mm_t(a, b):
    return lax.dot_general(a, b, (((0,), (0,)), ((), ())), preferred_element_type=F32)


def round_bf16(x, in_kernel):
    if in_kernel:
        return x.astype(BF16).astype(F32)
    return lax.reduce_precision(x, exponent_bits=8, mantissa_bits=7)


def id_column(ids, rows, in_kernel):
    if in_kernel:
        shape = (rows, ids.shape[1])
        eye = (lax.broadcasted_iota(jnp.int32, shape, 0) == lax.broadcasted_iota(jnp.int32, shape, 1))
        cols = lax.dot_general(eye.astype(BF16), ids, (((1,), (1,)), ((), ())), preferred_element_type=F32)
        return cols[:, 0:1]
    return ids.reshape(-1)[:rows].astype(F32)[:, None]


def hyena_math(pieces, spec1, spec2, mats, rows, wait, in_kernel):
    nseq = len(pieces)
    per = pieces[0].shape[1]
    length = nseq * rows
    half = length // 2
    order = [(nseq - j) % nseq for j in range(nseq)]
    segs = jnp.concatenate([id_column(pieces[k][2 * rows:, :], rows, in_kernel) for k in order], axis=0)
    m0 = (segs == 0).astype(F32)
    m1 = (segs == 1).astype(F32)
    first = jnp.concatenate([pieces[k][0:rows, :] for k in order], axis=0).astype(F32)
    gate = jnp.concatenate([pieces[k][rows:2 * rows, :] for k in order], axis=0).astype(F32)

    def conv(z, spec, first_call):
        masked = jnp.concatenate([z * m0, z * m1], axis=1).astype(BF16)
        if first_call:
            wait(0)
            wait(1)
        x = (jnp.dot(mats[0](), masked, preferred_element_type=F32)
             + jnp.dot(mats[1](), masked, preferred_element_type=F32))
        a, b, d = (jnp.concatenate([v, v], axis=1) for v in (f() for f in spec))
        xr = x[:half]
        xi = x[half:]
        row = lax.broadcasted_iota(jnp.int32, (length, 1), 0)
        weight = jnp.where((row == 0) | (row == half), 1.0 / length, 2.0 / length).astype(F32)
        y = jnp.concatenate([xr * a - xi * b, xr * b + xi * d], axis=0) * weight
        y_hi32 = round_bf16(y, in_kernel)
        y_hi = y_hi32.astype(BF16)
        y_lo = (y - y_hi32).astype(BF16)
        fhi = mats[0]()
        both = mm_t(fhi, y_hi) + mm_t(fhi, y_lo) + mm_t(mats[1](), y_hi)
        return both[:, :per] * m0 + both[:, per:] * m1

    first_mix = conv(first, spec1, True)
    second_input = round_bf16(gate * first_mix, in_kernel)
    return conv(second_input, spec2, False).astype(BF16)


def hyena_kernel(*refs, nseq, rows):
    pieces = [r[...] for r in refs[:nseq]]
    spec_refs = refs[nseq:nseq + 6]
    mats_hbm = refs[nseq + 6:nseq + 8]
    w_hbm = refs[nseq + 8]
    o_ref, w_out = refs[nseq + 9:nseq + 11]
    mats = refs[nseq + 11:nseq + 13]
    sem = refs[nseq + 13]
    copies = [pltpu.make_async_copy(mats_hbm[i], mats[i], sem.at[i]) for i in range(2)]
    w_copy = pltpu.make_async_copy(w_hbm, w_out, sem.at[2])
    for c in copies:
        c.start()
    w_copy.start()
    loader = lambda r: (lambda: r[...])
    spec1 = [loader(r) for r in spec_refs[:3]]
    spec2 = [loader(r) for r in spec_refs[3:]]
    o_ref[...] = hyena_math(pieces, spec1, spec2,
                            [loader(r) for r in mats], rows, lambda i: copies[i].wait(), True)
    w_copy.wait()


def hyena_call(pieces, spec1, spec2, mats, rows, out_weight):
    nseq = len(pieces)
    length = nseq * rows
    per = pieces[0].shape[1]
    if 4 * length * length * 2 > 8 * 1024 * 1024 or per < rows:
        const = lambda v: (lambda: v)
        return hyena_math(pieces, [const(v) for v in spec1], [const(v) for v in spec2],
                          [const(v) for v in mats], rows, lambda i: None, False), out_weight
    vmem = pl.BlockSpec(memory_space=pltpu.VMEM)
    hbm = pl.BlockSpec(memory_space=pltpu.MemorySpace.HBM)
    flops = 2 * (2 * length * length * 2 * per * 5)
    return pl.pallas_call(
        functools.partial(hyena_kernel, nseq=nseq, rows=rows),
        out_shape=(jax.ShapeDtypeStruct((length, per), BF16),
                   jax.ShapeDtypeStruct(out_weight.shape, out_weight.dtype)),
        in_specs=[vmem] * (nseq + 6) + [hbm] * 3,
        out_specs=(vmem, vmem),
        scratch_shapes=[pltpu.VMEM((length, length), BF16) for _ in range(2)]
        + [pltpu.SemaphoreType.DMA((3,))],
        compiler_params=pltpu.CompilerParams(vmem_limit_bytes=40 * 1024 * 1024),
        cost_estimate=pl.CostEstimate(flops=flops, transcendentals=0,
                                      bytes_accessed=4 * length * length * 2 + 8 * length * per),
    )(*pieces, *spec1, *spec2, *mats, out_weight)

def proj_kernel(*refs, nseq):
    src_ref = refs[0]
    pieces = refs[1:1 + nseq]
    w_ref = refs[1 + nseq]
    o_ref = refs[2 + nseq]
    per = pieces[0].shape[1]
    acc = None
    for k in range(nseq):
        start = pl.multiple_of(src_ref[k] * per, per)
        term = jnp.dot(pieces[k][...], w_ref[pl.ds(start, per), :], preferred_element_type=F32)
        acc = term if acc is None else acc + term
    o_ref[...] = acc


def proj_call(srcs, pieces, out_weight):
    nseq = len(pieces)
    rows, per = pieces[0].shape
    out_cols = out_weight.shape[1]
    vmem = pl.BlockSpec(memory_space=pltpu.VMEM)
    return pl.pallas_call(
        functools.partial(proj_kernel, nseq=nseq),
        out_shape=jax.ShapeDtypeStruct((rows, out_cols), F32),
        in_specs=[pl.BlockSpec(memory_space=pltpu.SMEM)] + [vmem] * (nseq + 1),
        out_specs=vmem,
        compiler_params=pltpu.CompilerParams(vmem_limit_bytes=24 * 1024 * 1024),
        cost_estimate=pl.CostEstimate(flops=2 * rows * per * nseq * out_cols, transcendentals=0,
                                      bytes_accessed=per * nseq * out_cols * 2 + rows * out_cols * 4),
    )(srcs, *pieces, out_weight)


def mm(a, b):
    return jnp.dot(a, b, preferred_element_type=F32)


def swap(x, bit):
    return lax.ppermute(x, "chan", [(c, c ^ bit) for c in range(4)])


def make_local(nseq, nchan):
    def local(value, first_gate, second_gate, first_filter, second_filter, out_weight, segment_ids):
        chans = value.shape[1]
        filt_local, length = first_filter.shape
        group = chans // filt_local
        per = chans // nseq
        fpd = per // group
        half = length // 2
        (f_hi, f_lo), (i_hi, i_lo) = dft_mats(length)
        f_hi, f_lo, i_hi, i_lo = (jnp.asarray(m) for m in (f_hi, f_lo, i_hi, i_lo))

        def spectrum(filt):
            mine = lax.dynamic_slice_in_dim(filt, me * fpd, fpd, 0)
            taps = jnp.repeat(mine.T, group, axis=1)
            spec = mm(f_hi, taps) + mm(f_lo, taps)
            re, im = spec[:half], spec[half:]
            row0 = lax.broadcasted_iota(jnp.int32, re.shape, 0) == 0
            a = re
            b = jnp.where(row0, 0.0, im)
            d = jnp.where(row0, im, re)
            return a, b, d

        rows = value.shape[0]
        me = lax.axis_index("seq")
        order = [0] + [k for k in (1, nseq - 1) if k < nseq] + [k for k in range(2, nseq - 1)]
        order = list(dict.fromkeys(order))

        first_input = (first_gate.astype(F32) * value.astype(F32)).astype(BF16)
        id_rows = -(-rows // per)
        pad_rows = -(-id_rows // 16) * 16
        ids = jnp.pad(segment_ids.astype(BF16), (0, pad_rows * per - rows)).reshape(pad_rows, per)

        def block_for(dest):
            cols = lambda x: lax.dynamic_slice_in_dim(x, dest * per, per, 1)
            return jnp.concatenate([cols(first_input), cols(second_gate), ids], axis=0)

        got = {0: block_for(me)}
        for k in order[1:]:
            got[k] = lax.ppermute(block_for((me + k) % nseq), "seq", [(i, (i + k) % nseq) for i in range(nseq)])
        second_mix, staged_weight = hyena_call(
            [got[k] for k in range(nseq)], spectrum(first_filter),
            spectrum(second_filter), (f_hi, f_lo), rows, out_weight)
        mix_pieces = {0: second_mix[:rows]}
        for k in order[1:]:
            mix_pieces[k] = lax.ppermute(second_mix[k * rows:(k + 1) * rows], "seq",
                                         [(i, (i + k) % nseq) for i in range(nseq)])
        out_cols = out_weight.shape[1]

        srcs = jnp.stack([((me - k) % nseq).astype(jnp.int32) for k in range(nseq)])
        partial_out = proj_call(srcs, [mix_pieces[k] for k in range(nseq)], staged_weight)

        if nchan != 4:
            return lax.psum(partial_out, "chan").astype(BF16)
        core = lax.axis_index("chan") % 2
        width = out_cols // 2
        other = lax.dynamic_slice_in_dim(partial_out, (1 - core) * width, width, 1)
        got_other = swap(other.astype(BF16), 1)
        mine = lax.dynamic_slice_in_dim(partial_out, core * width, width, 1)
        chip = mine + got_other.astype(F32)
        total = (chip + swap(chip.astype(BF16), 2).astype(F32)).astype(BF16)
        peer = swap(total, 1)
        return jnp.where(core == 0, jnp.concatenate([total, peer], 1), jnp.concatenate([peer, total], 1))

    return local


def solution(mesh):
    in_specs = (
        P(("groups", "seq"), "chan"),
        P(("groups", "seq"), "chan"),
        P(("groups", "seq"), "chan"),
        P("chan", None),
        P("chan", None),
        P("chan", None),
        P(("groups", "seq")),
    )
    out_specs = P(("groups", "seq"), None)
    local = make_local(mesh.shape["seq"], mesh.shape["chan"])
    return jax.shard_map(local, mesh=mesh, in_specs=in_specs, out_specs=out_specs, check_vma=False)
```

```python
import functools
import numpy as np
import jax
import jax.numpy as jnp
from jax import lax
from jax.sharding import PartitionSpec as P
from jax.experimental import pallas as pl
from jax.experimental.pallas import tpu as pltpu

F32 = jnp.float32
BF16 = jnp.bfloat16


def split_bf16(mat):
    hi = mat.astype(jnp.bfloat16)
    lo = (mat - hi.astype(np.float64)).astype(jnp.bfloat16)
    return hi, lo


def dft_mats(length):
    half = length // 2
    n = np.arange(length)
    f = np.arange(half)
    ang = 2.0 * np.pi * ((f[:, None] * n[None, :]) % length) / length
    fwd = np.zeros((length, length))
    fwd[:half] = np.cos(ang)
    fwd[half] = np.where(n % 2 == 0, 1.0, -1.0)
    fwd[half + 1:] = -np.sin(ang[1:])
    inv = np.zeros((length, length))
    scale = np.full(half, 2.0)
    scale[0] = 1.0
    inv[:, :half] = (np.cos(ang) * scale[:, None]).T / length
    inv[:, half] = np.where(n % 2 == 0, 1.0, -1.0) / length
    inv[:, half + 1:] = (-2.0 * np.sin(ang[1:])).T / length
    return split_bf16(fwd), split_bf16(inv)


def mm_t(a, b):
    return lax.dot_general(a, b, (((0,), (0,)), ((), ())), preferred_element_type=F32)


def round_bf16(x, in_kernel):
    if in_kernel:
        return x.astype(BF16).astype(F32)
    return lax.reduce_precision(x, exponent_bits=8, mantissa_bits=7)


def id_column(ids, rows, in_kernel):
    if in_kernel:
        shape = (rows, ids.shape[1])
        eye = (lax.broadcasted_iota(jnp.int32, shape, 0) == lax.broadcasted_iota(jnp.int32, shape, 1))
        cols = lax.dot_general(eye.astype(BF16), ids, (((1,), (1,)), ((), ())), preferred_element_type=F32)
        return cols[:, 0:1]
    return ids.reshape(-1)[:rows].astype(F32)[:, None]


def hyena_math(pieces, spec1, spec2, mats, rows, wait, in_kernel):
    nseq = len(pieces)
    per = pieces[0].shape[1]
    length = nseq * rows
    half = length // 2
    order = [(nseq - j) % nseq for j in range(nseq)]
    segs = jnp.concatenate([id_column(pieces[k][2 * rows:, :], rows, in_kernel) for k in order], axis=0)
    m0 = (segs == 0).astype(F32)
    m1 = (segs == 1).astype(F32)
    first = jnp.concatenate([pieces[k][0:rows, :] for k in order], axis=0).astype(F32)
    gate = jnp.concatenate([pieces[k][rows:2 * rows, :] for k in order], axis=0).astype(F32)

    def conv(z, spec, first_call):
        masked = jnp.concatenate([z * m0, z * m1], axis=1).astype(BF16)
        if first_call:
            wait(0)
            wait(1)
        x = (jnp.dot(mats[0](), masked, preferred_element_type=F32)
             + jnp.dot(mats[1](), masked, preferred_element_type=F32))
        a, b, d = (jnp.concatenate([v, v], axis=1) for v in (f() for f in spec))
        xr = x[:half]
        xi = x[half:]
        row = lax.broadcasted_iota(jnp.int32, (length, 1), 0)
        weight = jnp.where((row == 0) | (row == half), 1.0 / length, 2.0 / length).astype(F32)
        y = jnp.concatenate([xr * a - xi * b, xr * b + xi * d], axis=0) * weight
        y_hi32 = round_bf16(y, in_kernel)
        y_hi = y_hi32.astype(BF16)
        y_lo = (y - y_hi32).astype(BF16)
        fhi = mats[0]()
        both = mm_t(fhi, y_hi) + mm_t(fhi, y_lo) + mm_t(mats[1](), y_hi)
        return both[:, :per] * m0 + both[:, per:] * m1

    first_mix = conv(first, spec1, True)
    second_input = round_bf16(gate * first_mix, in_kernel)
    return conv(second_input, spec2, False).astype(BF16)


def hyena_kernel(*refs, nseq, rows):
    pieces = [r[...] for r in refs[:nseq]]
    spec_refs = refs[nseq:nseq + 6]
    mats_hbm = refs[nseq + 6:nseq + 8]
    w_hbm = refs[nseq + 8]
    o_ref, w_out = refs[nseq + 9:nseq + 11]
    mats = refs[nseq + 11:nseq + 13]
    sem = refs[nseq + 13]
    copies = [pltpu.make_async_copy(mats_hbm[i], mats[i], sem.at[i]) for i in range(2)]
    w_copy = pltpu.make_async_copy(w_hbm, w_out, sem.at[2])
    for c in copies:
        c.start()
    w_copy.start()
    loader = lambda r: (lambda: r[...])
    spec1 = [loader(r) for r in spec_refs[:3]]
    spec2 = [loader(r) for r in spec_refs[3:]]
    o_ref[...] = hyena_math(pieces, spec1, spec2,
                            [loader(r) for r in mats], rows, lambda i: copies[i].wait(), True)
    w_copy.wait()


def hyena_call(pieces, spec1, spec2, mats, rows, out_weight):
    nseq = len(pieces)
    length = nseq * rows
    per = pieces[0].shape[1]
    if 4 * length * length * 2 > 8 * 1024 * 1024 or per < rows:
        const = lambda v: (lambda: v)
        return hyena_math(pieces, [const(v) for v in spec1], [const(v) for v in spec2],
                          [const(v) for v in mats], rows, lambda i: None, False), out_weight
    vmem = pl.BlockSpec(memory_space=pltpu.VMEM)
    hbm = pl.BlockSpec(memory_space=pltpu.MemorySpace.HBM)
    flops = 2 * (2 * length * length * 2 * per * 5)
    return pl.pallas_call(
        functools.partial(hyena_kernel, nseq=nseq, rows=rows),
        out_shape=(jax.ShapeDtypeStruct((length, per), BF16),
                   jax.ShapeDtypeStruct(out_weight.shape, out_weight.dtype)),
        in_specs=[vmem] * (nseq + 6) + [hbm] * 3,
        out_specs=(vmem, vmem),
        scratch_shapes=[pltpu.VMEM((length, length), BF16) for _ in range(2)]
        + [pltpu.SemaphoreType.DMA((3,))],
        compiler_params=pltpu.CompilerParams(vmem_limit_bytes=40 * 1024 * 1024),
        cost_estimate=pl.CostEstimate(flops=flops, transcendentals=0,
                                      bytes_accessed=4 * length * length * 2 + 8 * length * per),
    )(*pieces, *spec1, *spec2, *mats, out_weight)

def proj_kernel(*refs, nseq):
    src_ref = refs[0]
    pieces = refs[1:1 + nseq]
    w_ref = refs[1 + nseq]
    o_ref = refs[2 + nseq]
    per = pieces[0].shape[1]
    acc = None
    for k in range(nseq):
        start = pl.multiple_of(src_ref[k] * per, per)
        term = jnp.dot(pieces[k][...], w_ref[pl.ds(start, per), :], preferred_element_type=F32)
        acc = term if acc is None else acc + term
    o_ref[...] = acc


def proj_call(srcs, pieces, out_weight):
    nseq = len(pieces)
    rows, per = pieces[0].shape
    out_cols = out_weight.shape[1]
    vmem = pl.BlockSpec(memory_space=pltpu.VMEM)
    return pl.pallas_call(
        functools.partial(proj_kernel, nseq=nseq),
        out_shape=jax.ShapeDtypeStruct((rows, out_cols), F32),
        in_specs=[pl.BlockSpec(memory_space=pltpu.SMEM)] + [vmem] * (nseq + 1),
        out_specs=vmem,
        compiler_params=pltpu.CompilerParams(vmem_limit_bytes=24 * 1024 * 1024),
        cost_estimate=pl.CostEstimate(flops=2 * rows * per * nseq * out_cols, transcendentals=0,
                                      bytes_accessed=per * nseq * out_cols * 2 + rows * out_cols * 4),
    )(srcs, *pieces, out_weight)


def mm(a, b):
    return jnp.dot(a, b, preferred_element_type=F32)


def swap(x, bit):
    return lax.ppermute(x, "chan", [(c, c ^ bit) for c in range(4)])


def make_local(nseq, nchan):
    def local(value, first_gate, second_gate, first_filter, second_filter, out_weight, segment_ids):
        chans = value.shape[1]
        filt_local, length = first_filter.shape
        group = chans // filt_local
        per = chans // nseq
        fpd = per // group
        half = length // 2
        (f_hi, f_lo), (i_hi, i_lo) = dft_mats(length)
        f_hi, f_lo, i_hi, i_lo = (jnp.asarray(m) for m in (f_hi, f_lo, i_hi, i_lo))

        def spectrum(filt):
            mine = lax.dynamic_slice_in_dim(filt, me * fpd, fpd, 0)
            taps = jnp.repeat(mine.T, group, axis=1)
            spec = mm(f_hi, taps) + mm(f_lo, taps)
            re, im = spec[:half], spec[half:]
            row0 = lax.broadcasted_iota(jnp.int32, re.shape, 0) == 0
            a = re
            b = jnp.where(row0, 0.0, im)
            d = jnp.where(row0, im, re)
            return a, b, d

        rows = value.shape[0]
        me = lax.axis_index("seq")
        order = [0] + [k for k in (1, nseq - 1) if k < nseq] + [k for k in range(2, nseq - 1)]
        order = list(dict.fromkeys(order))

        id_rows = -(-rows // per)
        pad_rows = -(-id_rows // 16) * 16

        def block_for(dest):
            cols = lambda x: lax.dynamic_slice_in_dim(x, dest * per, per, 1)
            first_input = (cols(first_gate).astype(F32) * cols(value).astype(F32)).astype(BF16)
            ids = jnp.pad(segment_ids.astype(BF16), (0, pad_rows * per - rows)).reshape(pad_rows, per)
            return jnp.concatenate([first_input, cols(second_gate), ids], axis=0)

        got = {0: block_for(me)}
        for k in order[1:]:
            got[k] = lax.ppermute(block_for((me + k) % nseq), "seq", [(i, (i + k) % nseq) for i in range(nseq)])
        second_mix, staged_weight = hyena_call(
            [got[k] for k in range(nseq)], spectrum(first_filter),
            spectrum(second_filter), (f_hi, f_lo), rows, out_weight)
        mix_pieces = {0: second_mix[:rows]}
        for k in order[1:]:
            mix_pieces[k] = lax.ppermute(second_mix[k * rows:(k + 1) * rows], "seq",
                                         [(i, (i + k) % nseq) for i in range(nseq)])
        out_cols = out_weight.shape[1]

        srcs = jnp.stack([((me - k) % nseq).astype(jnp.int32) for k in range(nseq)])
        partial_out = proj_call(srcs, [mix_pieces[k] for k in range(nseq)], staged_weight)

        if nchan != 4:
            return lax.psum(partial_out, "chan").astype(BF16)
        core = lax.axis_index("chan") % 2
        width = out_cols // 2
        other = lax.dynamic_slice_in_dim(partial_out, (1 - core) * width, width, 1)
        got_other = swap(other.astype(BF16), 1)
        mine = lax.dynamic_slice_in_dim(partial_out, core * width, width, 1)
        chip = mine + got_other.astype(F32)
        total = (chip + swap(chip.astype(BF16), 2).astype(F32)).astype(BF16)
        peer = swap(total, 1)
        return jnp.where(core == 0, jnp.concatenate([total, peer], 1), jnp.concatenate([peer, total], 1))

    return local


def solution(mesh):
    in_specs = (
        P(("groups", "seq"), "chan"),
        P(("groups", "seq"), "chan"),
        P(("groups", "seq"), "chan"),
        P("chan", None),
        P("chan", None),
        P("chan", None),
        P(("groups", "seq")),
    )
    out_specs = P(("groups", "seq"), None)
    local = make_local(mesh.shape["seq"], mesh.shape["chan"])
    return jax.shard_map(local, mesh=mesh, in_specs=in_specs, out_specs=out_specs, check_vma=False)
```

```python
import functools
import numpy as np
import jax
import jax.numpy as jnp
from jax import lax
from jax.sharding import PartitionSpec as P
from jax.experimental import pallas as pl
from jax.experimental.pallas import tpu as pltpu

F32 = jnp.float32
BF16 = jnp.bfloat16


def split_bf16(mat):
    hi = mat.astype(jnp.bfloat16)
    lo = (mat - hi.astype(np.float64)).astype(jnp.bfloat16)
    return hi, lo


def dft_mats(length):
    half = length // 2
    n = np.arange(length)
    f = np.arange(half)
    ang = 2.0 * np.pi * ((f[:, None] * n[None, :]) % length) / length
    fwd = np.zeros((length, length))
    fwd[:half] = np.cos(ang)
    fwd[half] = np.where(n % 2 == 0, 1.0, -1.0)
    fwd[half + 1:] = -np.sin(ang[1:])
    inv = np.zeros((length, length))
    scale = np.full(half, 2.0)
    scale[0] = 1.0
    inv[:, :half] = (np.cos(ang) * scale[:, None]).T / length
    inv[:, half] = np.where(n % 2 == 0, 1.0, -1.0) / length
    inv[:, half + 1:] = (-2.0 * np.sin(ang[1:])).T / length
    return split_bf16(fwd), split_bf16(inv)


def mm_t(a, b):
    return lax.dot_general(a, b, (((0,), (0,)), ((), ())), preferred_element_type=F32)


def round_bf16(x, in_kernel):
    if in_kernel:
        return x.astype(BF16).astype(F32)
    return lax.reduce_precision(x, exponent_bits=8, mantissa_bits=7)


def id_column(ids, rows, in_kernel):
    if in_kernel:
        shape = (rows, ids.shape[1])
        eye = (lax.broadcasted_iota(jnp.int32, shape, 0) == lax.broadcasted_iota(jnp.int32, shape, 1))
        cols = lax.dot_general(eye.astype(BF16), ids, (((1,), (1,)), ((), ())), preferred_element_type=F32)
        return cols[:, 0:1]
    return ids.reshape(-1)[:rows].astype(F32)[:, None]


def hyena_math(pieces, spec1, spec2, mats, rows, wait, in_kernel):
    nseq = len(pieces)
    per = pieces[0].shape[1]
    length = nseq * rows
    half = length // 2
    order = [(nseq - j) % nseq for j in range(nseq)]
    segs = jnp.concatenate([id_column(pieces[k][2 * rows:, :], rows, in_kernel) for k in order], axis=0)
    m0 = (segs == 0).astype(F32)
    m1 = (segs == 1).astype(F32)
    first = jnp.concatenate([pieces[k][0:rows, :] for k in order], axis=0).astype(F32)
    gate = jnp.concatenate([pieces[k][rows:2 * rows, :] for k in order], axis=0).astype(F32)

    def conv(z, spec, first_call):
        masked = jnp.concatenate([z * m0, z * m1], axis=1).astype(BF16)
        if first_call:
            wait(0)
            wait(1)
        x = (jnp.dot(mats[0](), masked, preferred_element_type=F32)
             + jnp.dot(mats[1](), masked, preferred_element_type=F32))
        a, b, d = (jnp.concatenate([v, v], axis=1) for v in (f() for f in spec))
        xr = x[:half]
        xi = x[half:]
        row = lax.broadcasted_iota(jnp.int32, (length, 1), 0)
        weight = jnp.where((row == 0) | (row == half), 1.0 / length, 2.0 / length).astype(F32)
        y = jnp.concatenate([xr * a - xi * b, xr * b + xi * d], axis=0) * weight
        y_hi32 = round_bf16(y, in_kernel)
        y_hi = y_hi32.astype(BF16)
        y_lo = (y - y_hi32).astype(BF16)
        fhi = mats[0]()
        both = mm_t(fhi, y_hi) + mm_t(fhi, y_lo) + mm_t(mats[1](), y_hi)
        return both[:, :per] * m0 + both[:, per:] * m1

    first_mix = conv(first, spec1, True)
    second_input = round_bf16(gate * first_mix, in_kernel)
    return conv(second_input, spec2, False).astype(BF16)


def hyena_kernel(*refs, nseq, rows):
    pieces = [r[...] for r in refs[:nseq]]
    spec_refs = refs[nseq:nseq + 6]
    mats_hbm = refs[nseq + 6:nseq + 8]
    w_hbm = refs[nseq + 8]
    o_ref, w_out = refs[nseq + 9:nseq + 11]
    mats = refs[nseq + 11:nseq + 13]
    sem = refs[nseq + 13]
    copies = [pltpu.make_async_copy(mats_hbm[i], mats[i], sem.at[i]) for i in range(2)]
    w_copy = pltpu.make_async_copy(w_hbm, w_out, sem.at[2])
    for c in copies:
        c.start()
    w_copy.start()
    loader = lambda r: (lambda: r[...])
    spec1 = [loader(r) for r in spec_refs[:3]]
    spec2 = [loader(r) for r in spec_refs[3:]]
    o_ref[...] = hyena_math(pieces, spec1, spec2,
                            [loader(r) for r in mats], rows, lambda i: copies[i].wait(), True)
    w_copy.wait()


def hyena_call(pieces, spec1, spec2, mats, rows, out_weight):
    nseq = len(pieces)
    length = nseq * rows
    per = pieces[0].shape[1]
    if 4 * length * length * 2 > 8 * 1024 * 1024 or per < rows:
        const = lambda v: (lambda: v)
        return hyena_math(pieces, [const(v) for v in spec1], [const(v) for v in spec2],
                          [const(v) for v in mats], rows, lambda i: None, False), out_weight
    vmem = pl.BlockSpec(memory_space=pltpu.VMEM)
    hbm = pl.BlockSpec(memory_space=pltpu.MemorySpace.HBM)
    flops = 2 * (2 * length * length * 2 * per * 5)
    return pl.pallas_call(
        functools.partial(hyena_kernel, nseq=nseq, rows=rows),
        out_shape=(jax.ShapeDtypeStruct((length, per), BF16),
                   jax.ShapeDtypeStruct(out_weight.shape, out_weight.dtype)),
        in_specs=[vmem] * (nseq + 6) + [hbm] * 3,
        out_specs=(vmem, vmem),
        scratch_shapes=[pltpu.VMEM((length, length), BF16) for _ in range(2)]
        + [pltpu.SemaphoreType.DMA((3,))],
        compiler_params=pltpu.CompilerParams(vmem_limit_bytes=40 * 1024 * 1024),
        cost_estimate=pl.CostEstimate(flops=flops, transcendentals=0,
                                      bytes_accessed=4 * length * length * 2 + 8 * length * per),
    )(*pieces, *spec1, *spec2, *mats, out_weight)

def proj_kernel(*refs, nseq):
    src_ref = refs[0]
    pieces = refs[1:1 + nseq]
    w_ref = refs[1 + nseq]
    o_ref = refs[2 + nseq]
    per = pieces[0].shape[1]
    width = o_ref.shape[1]
    col = pl.multiple_of(src_ref[nseq] * width, width)
    acc = None
    for k in range(nseq):
        start = pl.multiple_of(src_ref[k] * per, per)
        term = jnp.dot(pieces[k][...], w_ref[pl.ds(start, per), pl.ds(col, width)],
                       preferred_element_type=F32)
        acc = term if acc is None else acc + term
    o_ref[...] = acc


def proj_call(srcs, pieces, out_weight, half=None):
    nseq = len(pieces)
    rows, per = pieces[0].shape
    out_cols = out_weight.shape[1]
    if half is None:
        srcs = jnp.concatenate([srcs, jnp.zeros((1,), jnp.int32)])
    else:
        out_cols = out_cols // 2
        srcs = jnp.concatenate([srcs, jnp.reshape(half, (1,)).astype(jnp.int32)])
    vmem = pl.BlockSpec(memory_space=pltpu.VMEM)
    return pl.pallas_call(
        functools.partial(proj_kernel, nseq=nseq),
        out_shape=jax.ShapeDtypeStruct((rows, out_cols), F32),
        in_specs=[pl.BlockSpec(memory_space=pltpu.SMEM)] + [vmem] * (nseq + 1),
        out_specs=vmem,
        compiler_params=pltpu.CompilerParams(vmem_limit_bytes=24 * 1024 * 1024),
        cost_estimate=pl.CostEstimate(flops=2 * rows * per * nseq * out_cols, transcendentals=0,
                                      bytes_accessed=per * nseq * out_cols * 2 + rows * out_cols * 4),
    )(srcs, *pieces, out_weight)


def mm(a, b):
    return jnp.dot(a, b, preferred_element_type=F32)


def swap(x, bit):
    return lax.ppermute(x, "chan", [(c, c ^ bit) for c in range(4)])


def make_local(nseq, nchan):
    def local(value, first_gate, second_gate, first_filter, second_filter, out_weight, segment_ids):
        chans = value.shape[1]
        filt_local, length = first_filter.shape
        group = chans // filt_local
        per = chans // nseq
        fpd = per // group
        half = length // 2
        (f_hi, f_lo), (i_hi, i_lo) = dft_mats(length)
        f_hi, f_lo, i_hi, i_lo = (jnp.asarray(m) for m in (f_hi, f_lo, i_hi, i_lo))

        def spectrum(filt):
            mine = lax.dynamic_slice_in_dim(filt, me * fpd, fpd, 0)
            taps = jnp.repeat(mine.T, group, axis=1)
            spec = mm(f_hi, taps) + mm(f_lo, taps)
            re, im = spec[:half], spec[half:]
            row0 = lax.broadcasted_iota(jnp.int32, re.shape, 0) == 0
            a = re
            b = jnp.where(row0, 0.0, im)
            d = jnp.where(row0, im, re)
            return a, b, d

        rows = value.shape[0]
        me = lax.axis_index("seq")
        order = [0] + [k for k in (1, nseq - 1) if k < nseq] + [k for k in range(2, nseq - 1)]
        order = list(dict.fromkeys(order))

        id_rows = -(-rows // per)
        pad_rows = -(-id_rows // 16) * 16

        def block_for(dest):
            cols = lambda x: lax.dynamic_slice_in_dim(x, dest * per, per, 1)
            first_input = (cols(first_gate).astype(F32) * cols(value).astype(F32)).astype(BF16)
            ids = jnp.pad(segment_ids.astype(BF16), (0, pad_rows * per - rows)).reshape(pad_rows, per)
            return jnp.concatenate([first_input, cols(second_gate), ids], axis=0)

        got = {0: block_for(me)}
        for k in order[1:]:
            got[k] = lax.ppermute(block_for((me + k) % nseq), "seq", [(i, (i + k) % nseq) for i in range(nseq)])
        second_mix, staged_weight = hyena_call(
            [got[k] for k in range(nseq)], spectrum(first_filter),
            spectrum(second_filter), (f_hi, f_lo), rows, out_weight)
        mix_pieces = {0: second_mix[:rows]}
        for k in order[1:]:
            mix_pieces[k] = lax.ppermute(second_mix[k * rows:(k + 1) * rows], "seq",
                                         [(i, (i + k) % nseq) for i in range(nseq)])
        out_cols = out_weight.shape[1]

        srcs = jnp.stack([((me - k) % nseq).astype(jnp.int32) for k in range(nseq)])
        received = [mix_pieces[k] for k in range(nseq)]
        if nchan != 4:
            return lax.psum(proj_call(srcs, received, staged_weight), "chan").astype(BF16)
        core = lax.axis_index("chan") % 2
        other = proj_call(srcs, received, staged_weight, 1 - core)
        got_other = swap(other.astype(BF16), 1)
        mine = proj_call(srcs, received, staged_weight, core)
        chip = mine + got_other.astype(F32)
        total = (chip + swap(chip.astype(BF16), 2).astype(F32)).astype(BF16)
        peer = swap(total, 1)
        return jnp.where(core == 0, jnp.concatenate([total, peer], 1), jnp.concatenate([peer, total], 1))

    return local


def solution(mesh):
    in_specs = (
        P(("groups", "seq"), "chan"),
        P(("groups", "seq"), "chan"),
        P(("groups", "seq"), "chan"),
        P("chan", None),
        P("chan", None),
        P("chan", None),
        P(("groups", "seq")),
    )
    out_specs = P(("groups", "seq"), None)
    local = make_local(mesh.shape["seq"], mesh.shape["chan"])
    return jax.shard_map(local, mesh=mesh, in_specs=in_specs, out_specs=out_specs, check_vma=False)
```

```python
import functools
import numpy as np
import jax
import jax.numpy as jnp
from jax import lax
from jax.sharding import PartitionSpec as P
from jax.experimental import pallas as pl
from jax.experimental.pallas import tpu as pltpu

F32 = jnp.float32
BF16 = jnp.bfloat16


def split_bf16(mat):
    hi = mat.astype(jnp.bfloat16)
    lo = (mat - hi.astype(np.float64)).astype(jnp.bfloat16)
    return hi, lo


def dft_mats(length):
    half = length // 2
    n = np.arange(length)
    f = np.arange(half)
    ang = 2.0 * np.pi * ((f[:, None] * n[None, :]) % length) / length
    fwd = np.zeros((length, length))
    fwd[:half] = np.cos(ang)
    fwd[half] = np.where(n % 2 == 0, 1.0, -1.0)
    fwd[half + 1:] = -np.sin(ang[1:])
    inv = np.zeros((length, length))
    scale = np.full(half, 2.0)
    scale[0] = 1.0
    inv[:, :half] = (np.cos(ang) * scale[:, None]).T / length
    inv[:, half] = np.where(n % 2 == 0, 1.0, -1.0) / length
    inv[:, half + 1:] = (-2.0 * np.sin(ang[1:])).T / length
    return split_bf16(fwd), split_bf16(inv)


def mm_t(a, b):
    return lax.dot_general(a, b, (((0,), (0,)), ((), ())), preferred_element_type=F32)


def round_bf16(x, in_kernel):
    if in_kernel:
        return x.astype(BF16).astype(F32)
    return lax.reduce_precision(x, exponent_bits=8, mantissa_bits=7)


def id_column(ids, rows, in_kernel):
    if in_kernel:
        shape = (rows, ids.shape[1])
        eye = (lax.broadcasted_iota(jnp.int32, shape, 0) == lax.broadcasted_iota(jnp.int32, shape, 1))
        cols = lax.dot_general(eye.astype(BF16), ids, (((1,), (1,)), ((), ())), preferred_element_type=F32)
        return cols[:, 0:1]
    return ids.reshape(-1)[:rows].astype(F32)[:, None]


def hyena_math(pieces, spec1, spec2, mats, rows, wait, in_kernel):
    nseq = len(pieces)
    per = pieces[0].shape[1]
    length = nseq * rows
    half = length // 2
    order = [(nseq - j) % nseq for j in range(nseq)]
    segs = jnp.concatenate([id_column(pieces[k][2 * rows:, :], rows, in_kernel) for k in order], axis=0)
    m0 = (segs == 0).astype(F32)
    m1 = (segs == 1).astype(F32)
    first = jnp.concatenate([pieces[k][0:rows, :] for k in order], axis=0).astype(F32)
    gate = jnp.concatenate([pieces[k][rows:2 * rows, :] for k in order], axis=0).astype(F32)

    def conv(z, spec, first_call):
        masked = jnp.concatenate([z * m0, z * m1], axis=1).astype(BF16)
        if first_call:
            wait(0)
            wait(1)
        x = (jnp.dot(mats[0](), masked, preferred_element_type=F32)
             + jnp.dot(mats[1](), masked, preferred_element_type=F32))
        a, b, d = (jnp.concatenate([v, v], axis=1) for v in (f() for f in spec))
        xr = x[:half]
        xi = x[half:]
        row = lax.broadcasted_iota(jnp.int32, (length, 1), 0)
        weight = jnp.where((row == 0) | (row == half), 1.0 / length, 2.0 / length).astype(F32)
        y = jnp.concatenate([xr * a - xi * b, xr * b + xi * d], axis=0) * weight
        y_hi32 = round_bf16(y, in_kernel)
        y_hi = y_hi32.astype(BF16)
        y_lo = (y - y_hi32).astype(BF16)
        fhi = mats[0]()
        both = mm_t(fhi, y_hi) + mm_t(fhi, y_lo) + mm_t(mats[1](), y_hi)
        return both[:, :per] * m0 + both[:, per:] * m1

    first_mix = conv(first, spec1, True)
    second_input = round_bf16(gate * first_mix, in_kernel)
    return conv(second_input, spec2, False).astype(BF16)


def hyena_kernel(*refs, nseq, rows):
    pieces = [r[...] for r in refs[:nseq]]
    spec_refs = refs[nseq:nseq + 6]
    mats_hbm = refs[nseq + 6:nseq + 8]
    w_hbm = refs[nseq + 8]
    o_ref, w_out = refs[nseq + 9:nseq + 11]
    mats = refs[nseq + 11:nseq + 13]
    sem = refs[nseq + 13]
    copies = [pltpu.make_async_copy(mats_hbm[i], mats[i], sem.at[i]) for i in range(2)]
    w_copy = pltpu.make_async_copy(w_hbm, w_out, sem.at[2])
    for c in copies:
        c.start()
    w_copy.start()
    loader = lambda r: (lambda: r[...])
    spec1 = [loader(r) for r in spec_refs[:3]]
    spec2 = [loader(r) for r in spec_refs[3:]]
    o_ref[...] = hyena_math(pieces, spec1, spec2,
                            [loader(r) for r in mats], rows, lambda i: copies[i].wait(), True)
    w_copy.wait()


def hyena_call(pieces, spec1, spec2, mats, rows, out_weight):
    nseq = len(pieces)
    length = nseq * rows
    per = pieces[0].shape[1]
    if 4 * length * length * 2 > 8 * 1024 * 1024 or per < rows:
        const = lambda v: (lambda: v)
        return hyena_math(pieces, [const(v) for v in spec1], [const(v) for v in spec2],
                          [const(v) for v in mats], rows, lambda i: None, False), out_weight
    vmem = pl.BlockSpec(memory_space=pltpu.VMEM)
    hbm = pl.BlockSpec(memory_space=pltpu.MemorySpace.HBM)
    flops = 2 * (2 * length * length * 2 * per * 5)
    return pl.pallas_call(
        functools.partial(hyena_kernel, nseq=nseq, rows=rows),
        out_shape=(jax.ShapeDtypeStruct((length, per), BF16),
                   jax.ShapeDtypeStruct(out_weight.shape, out_weight.dtype)),
        in_specs=[vmem] * (nseq + 6) + [hbm] * 3,
        out_specs=(vmem, vmem),
        scratch_shapes=[pltpu.VMEM((length, length), BF16) for _ in range(2)]
        + [pltpu.SemaphoreType.DMA((3,))],
        compiler_params=pltpu.CompilerParams(vmem_limit_bytes=40 * 1024 * 1024),
        cost_estimate=pl.CostEstimate(flops=flops, transcendentals=0,
                                      bytes_accessed=4 * length * length * 2 + 8 * length * per),
    )(*pieces, *spec1, *spec2, *mats, out_weight)

def proj_kernel(*refs, nseq):
    src_ref = refs[0]
    pieces = refs[1:1 + nseq]
    w_ref = refs[1 + nseq]
    o_ref = refs[2 + nseq]
    per = pieces[0].shape[1]
    acc = None
    for k in range(nseq):
        start = pl.multiple_of(src_ref[k] * per, per)
        term = jnp.dot(pieces[k][...], w_ref[pl.ds(start, per), :], preferred_element_type=F32)
        acc = term if acc is None else acc + term
    o_ref[...] = acc


def proj_call(srcs, pieces, out_weight):
    nseq = len(pieces)
    rows, per = pieces[0].shape
    out_cols = out_weight.shape[1]
    vmem = pl.BlockSpec(memory_space=pltpu.VMEM)
    return pl.pallas_call(
        functools.partial(proj_kernel, nseq=nseq),
        out_shape=jax.ShapeDtypeStruct((rows, out_cols), F32),
        in_specs=[pl.BlockSpec(memory_space=pltpu.SMEM)] + [vmem] * (nseq + 1),
        out_specs=vmem,
        compiler_params=pltpu.CompilerParams(vmem_limit_bytes=24 * 1024 * 1024),
        cost_estimate=pl.CostEstimate(flops=2 * rows * per * nseq * out_cols, transcendentals=0,
                                      bytes_accessed=per * nseq * out_cols * 2 + rows * out_cols * 4),
    )(srcs, *pieces, out_weight)


def mm(a, b):
    return jnp.dot(a, b, preferred_element_type=F32)


def swap(x, bit):
    return lax.ppermute(x, "chan", [(c, c ^ bit) for c in range(4)])


def make_local(nseq, nchan):
    def local(value, first_gate, second_gate, first_filter, second_filter, out_weight, segment_ids):
        chans = value.shape[1]
        filt_local, length = first_filter.shape
        group = chans // filt_local
        per = chans // nseq
        fpd = per // group
        half = length // 2
        (f_hi, f_lo), (i_hi, i_lo) = dft_mats(length)
        f_hi, f_lo, i_hi, i_lo = (jnp.asarray(m) for m in (f_hi, f_lo, i_hi, i_lo))

        def spectrum(filt):
            mine = lax.dynamic_slice_in_dim(filt, me * fpd, fpd, 0)
            taps = jnp.repeat(mine.T, group, axis=1)
            spec = mm(f_hi, taps) + mm(f_lo, taps)
            re, im = spec[:half], spec[half:]
            row0 = lax.broadcasted_iota(jnp.int32, re.shape, 0) == 0
            a = re
            b = jnp.where(row0, 0.0, im)
            d = jnp.where(row0, im, re)
            return a, b, d

        rows = value.shape[0]
        me = lax.axis_index("seq")
        order = [0] + [k for k in (1, nseq - 1) if k < nseq] + [k for k in range(2, nseq - 1)]
        order = list(dict.fromkeys(order))

        id_rows = -(-rows // per)
        pad_rows = -(-id_rows // 16) * 16

        def block_for(dest):
            cols = lambda x: lax.dynamic_slice_in_dim(x, dest * per, per, 1)
            first_input = (cols(first_gate).astype(F32) * cols(value).astype(F32)).astype(BF16)
            ids = jnp.pad(segment_ids.astype(BF16), (0, pad_rows * per - rows)).reshape(pad_rows, per)
            return jnp.concatenate([first_input, cols(second_gate), ids], axis=0)

        got = {0: block_for(me)}
        for k in order[1:]:
            got[k] = lax.ppermute(block_for((me + k) % nseq), "seq", [(i, (i + k) % nseq) for i in range(nseq)])
        second_mix, staged_weight = hyena_call(
            [got[k] for k in range(nseq)], spectrum(first_filter),
            spectrum(second_filter), (f_hi, f_lo), rows, out_weight)
        mix_pieces = {0: second_mix[:rows]}
        for k in order[1:]:
            mix_pieces[k] = lax.ppermute(second_mix[k * rows:(k + 1) * rows], "seq",
                                         [(i, (i + k) % nseq) for i in range(nseq)])
        out_cols = out_weight.shape[1]

        srcs = jnp.stack([((me - k) % nseq).astype(jnp.int32) for k in range(nseq)])
        partial_out = proj_call(srcs, [mix_pieces[k] for k in range(nseq)], staged_weight)

        if nchan != 4:
            return lax.psum(partial_out, "chan").astype(BF16)
        core = lax.axis_index("chan") % 2
        width = out_cols // 2
        other = lax.dynamic_slice_in_dim(partial_out, (1 - core) * width, width, 1)
        got_other = swap(other.astype(BF16), 1)
        mine = lax.dynamic_slice_in_dim(partial_out, core * width, width, 1)
        chip = mine + got_other.astype(F32)
        total = (chip + swap(chip.astype(BF16), 2).astype(F32)).astype(BF16)
        peer = swap(total, 1)
        first_half = core == 0
        return jnp.concatenate([jnp.where(first_half, total, peer), jnp.where(first_half, peer, total)], 1)

    return local


def solution(mesh):
    in_specs = (
        P(("groups", "seq"), "chan"),
        P(("groups", "seq"), "chan"),
        P(("groups", "seq"), "chan"),
        P("chan", None),
        P("chan", None),
        P("chan", None),
        P(("groups", "seq")),
    )
    out_specs = P(("groups", "seq"), None)
    local = make_local(mesh.shape["seq"], mesh.shape["chan"])
    return jax.shard_map(local, mesh=mesh, in_specs=in_specs, out_specs=out_specs, check_vma=False)
```
